32 devices in a mesh: groups: 2 (over x), outer: 16 (over z, y, core).
Axes of the slice: x: 2, y: 2, z: 4, core: 2. Of those that a mesh axis runs over, the one named last changes fastest.
Arguments:
- queries: bfloat16 [12288, 2048], P(('groups', 'outer')), parts along dimension 0, may hold values from -256 to 256, as said below
- key_rows: bfloat16 [12288, 2048], P(('groups', 'outer')), parts along dimension 0, may hold values from -4 to 4
- value_rows: bfloat16 [12288, 2048], P(('groups', 'outer')), parts along dimension 0, may hold values from -6 to 6
- widths: int32 [96], P(('groups', 'outer')), parts along dimension 0, may hold values from 1 to 4, as said below
- columns: int32 [32, 4, 1], P('groups'), parts along dimension 0, may hold values from 0 to 47, as said below
Outputs:
- context: bfloat16 [12288, 2048], P(('groups', 'outer')), parts along dimension 0
The draws below stay inside these ranges and needn't reach their ends.
There are 2 independent parts, one for each index of `groups`. The reference program is written for one: setup_inputs(seed, part) draws one part's arguments, and reference() takes and returns one part's arrays. A program takes and returns all parts, laid end to end along the dimension named above; each array names one. Nothing has to cross between parts.
Inputs may be any that keep to these rules, and one draw needn't show every extreme that they name: Block rows 3 and 4 have widths 4 and 1. columns[p, b, 0] is one block of panel p XOR 2**b, given by its index in the whole sequence. `queries`: entries of order one in most rows.
All inputs are finite; a program needn't handle non-finite values.
Results may differ from the reference program's by a relative error of at most 0.0022.
Values may be sent and summed in bfloat16 or wider, within the bound.
No kernel may reach another device: no remote copies, remote signals or barrier semaphores. Data moves between devices by JAX's collectives and lax.ppermute only.
A program may use at most 128 MiB of HBM per device.

```python
import math
import jax
import jax.numpy as jnp
from jax import lax

HEADS = 16
HDIM = 128
BLK = 128
WIN = 4
KSEL = 1
PANEL = 3
PANELS = 16
NB = 48
SEQ = 6144
LEVELS = 4
FEAT = 2048


def draw_queries(key, part):
    entries = jnp.clip(jax.random.normal(jax.random.fold_in(key, 11), (SEQ, HEADS, HDIM), jnp.float32), -4.0, 4.0)
    spread = jnp.exp(jax.random.uniform(jax.random.fold_in(key, 12), (SEQ, HEADS, 1), jnp.float32, 0.0, math.log(4.0)))
    values = entries * spread
    return values.reshape(SEQ, HEADS * HDIM).astype(jnp.bfloat16)


def draw_key_rows(key, part):
    values = jnp.clip(jax.random.normal(jax.random.fold_in(key, 13), (SEQ, HEADS, HDIM), jnp.float32), -4.0, 4.0)
    return values.reshape(SEQ, HEADS * HDIM).astype(jnp.bfloat16)


def draw_widths(key, part):
    drawn = jax.random.randint(jax.random.fold_in(key, 21), (NB,), 1, WIN + 1, jnp.int32)
    blocks = jnp.arange(NB, dtype=jnp.int32)
    drawn = jnp.where(blocks == PANEL, WIN, drawn)
    return jnp.where(blocks == PANEL + 1, 1, drawn).astype(jnp.int32)


def draw_columns(key, part):
    slot_ids = jnp.arange(PANEL, dtype=jnp.int32)
    ranked = jax.random.randint(jax.random.fold_in(key, 31), (PANELS, LEVELS, PANEL), 0, 1 << 20, jnp.int32) * PANEL + slot_ids
    panel_grid = jnp.arange(PANELS, dtype=jnp.int32)[:, None, None]
    level_grid = jnp.arange(LEVELS, dtype=jnp.int32)[None, :, None]
    force_low = (panel_grid == 1) & (level_grid == 0) & (slot_ids[None, None, :] == 0)
    force_high = (panel_grid == PANELS - 2) & (level_grid == 0) & (slot_ids[None, None, :] == PANEL - 1)
    ranked = jnp.where(force_low | force_high, -1, ranked)
    ordering = jnp.argsort(ranked, axis=-1)
    picked = ordering[..., :KSEL].astype(jnp.int32)
    panel_ids = jnp.arange(PANELS, dtype=jnp.int32)[:, None]
    strides = (2 ** jnp.arange(LEVELS, dtype=jnp.int32))[None, :]
    partner = jnp.bitwise_xor(panel_ids, strides)
    return (partner[:, :, None] * PANEL + picked).astype(jnp.int32)


def block_scale(rng, dims, cuts, least, top_value):
    gain = 1.0
    for position, parts in cuts:
        heights = jax.random.uniform(jax.random.fold_in(jax.random.fold_in(rng, 6), position), (parts,), jnp.float32, least / len(cuts), top_value / len(cuts))
        gain = gain * jnp.repeat(jnp.exp(heights), dims[position] // parts).reshape((-1,) + (1,) * (len(dims) - 1 - position))
    return gain


def centred(own_key, dims, scale, most, shards=(), held_as=jnp.bfloat16):
    result = jax.random.normal(own_key, dims, jnp.float32) * scale
    if len(shards) > 0:
        result = block_scale(own_key, dims, shards, -0.22, 0.18) * result
    return jnp.clip(result, min=-most, max=most).astype(held_as)


def setup_inputs(seed: int = 0, part: int = 0) -> dict:
    streams_of = jax.random.split(jax.random.key(seed), 6)
    part_keys = jax.random.split(jax.random.fold_in(streams_of[5], part), 6)
    queries = draw_queries(jax.random.fold_in(jax.random.fold_in(streams_of[5], part), 71), part)
    key_rows = draw_key_rows(jax.random.fold_in(jax.random.fold_in(streams_of[5], part), 71), part)
    value_rows = centred(part_keys[2], (SEQ, FEAT), 1.0, 6.0, ((0, 16),))
    widths = draw_widths(jax.random.fold_in(jax.random.fold_in(streams_of[5], part), 71), part)
    columns = draw_columns(jax.random.fold_in(jax.random.fold_in(streams_of[5], part), 71), part)
    return {"queries": queries, "key_rows": key_rows, "value_rows": value_rows, "widths": widths, "columns": columns}


def window_visible(widths, first_block, block_len, window):
    row_count = widths.shape[0]
    offsets = jnp.arange(window * block_len, dtype=jnp.int32) // block_len
    key_pos = jnp.arange(window * block_len, dtype=jnp.int32) % block_len
    query_pos = jnp.arange(block_len, dtype=jnp.int32)
    block_ids = first_block + jnp.arange(row_count, dtype=jnp.int32)
    inside = offsets[None, None, :] < widths[:, None, None]
    started = (block_ids[:, None, None] - offsets[None, None, :]) >= 0
    causal = (offsets[None, None, :] > 0) | (key_pos[None, None, :] <= query_pos[None, :, None])
    return inside & started & causal


def soft_group(scores, visible, value_block, einsum_form):
    if visible is None:
        masked = scores
    else:
        masked = jnp.where(visible, scores, -jnp.inf)
    row_max = jnp.max(masked, axis=-1)
    weights = jnp.exp(masked - row_max[..., None])
    row_total = jnp.sum(weights, axis=-1)
    rounded = lax.optimization_barrier(weights.astype(jnp.bfloat16)).astype(jnp.float32)
    summed = jnp.einsum(einsum_form, rounded, value_block.astype(jnp.float32))
    return row_max, row_total, summed


def merge_parts(first, second):
    row_max = jnp.maximum(first[0], second[0])
    first_factor = jnp.exp(first[0] - row_max)
    second_factor = jnp.exp(second[0] - row_max)
    return (row_max,
            first[1] * first_factor + second[1] * second_factor,
            first[2] * first_factor[..., None] + second[2] * second_factor[..., None])


def reference(queries, key_rows, value_rows, widths, columns):
    token_count = PANEL * BLK
    rim_len = (WIN - 1) * BLK
    features = HEADS * HDIM
    padded_keys = jnp.concatenate([jnp.zeros((rim_len, features), key_rows.dtype), key_rows], axis=0)
    padded_values = jnp.concatenate([jnp.zeros((rim_len, features), value_rows.dtype), value_rows], axis=0)
    score_scale = HDIM ** -0.5

    def window_stack(extended):
        return jnp.concatenate([extended[(WIN - 1 - offset) * BLK:(WIN - 1 - offset) * BLK + token_count].reshape(PANEL, BLK, HEADS, HDIM) for offset in range(WIN)], axis=1)

    def one_panel(panel_id):
        start = (panel_id * token_count).astype(jnp.int32)
        query_rows = lax.dynamic_slice_in_dim(queries, start, token_count, 0).astype(jnp.float32)
        ext_keys = lax.dynamic_slice_in_dim(padded_keys, start, rim_len + token_count, 0).astype(jnp.float32)
        ext_values = lax.dynamic_slice_in_dim(padded_values, start, rim_len + token_count, 0).astype(jnp.float32)
        query_four = query_rows.reshape(PANEL, BLK, HEADS, HDIM)
        scores = jnp.einsum("pqhd,pkhd->pqhk", query_four, window_stack(ext_keys)) * score_scale
        first_block = (panel_id * PANEL).astype(jnp.int32)
        panel_widths = lax.dynamic_slice_in_dim(widths, first_block, PANEL, 0)
        visible = window_visible(panel_widths, first_block, BLK, WIN)
        row_max, row_total, summed = soft_group(scores, visible[:, :, None, :], window_stack(ext_values), "pqhk,pkhd->pqhd")
        running = (row_max.reshape(token_count, HEADS), row_total.reshape(token_count, HEADS), summed.reshape(token_count, HEADS, HDIM))
        query_three = query_rows.reshape(token_count, HEADS, HDIM)
        for level_bit in range(LEVELS):
            blocks = columns[panel_id, level_bit]
            far_keys = jnp.concatenate([lax.dynamic_slice_in_dim(key_rows, (blocks[slot_index] * BLK).astype(jnp.int32), BLK, 0) for slot_index in range(KSEL)], axis=0)
            far_values = jnp.concatenate([lax.dynamic_slice_in_dim(value_rows, (blocks[slot_index] * BLK).astype(jnp.int32), BLK, 0) for slot_index in range(KSEL)], axis=0)
            far_scores = jnp.einsum("qhd,khd->qhk", query_three, far_keys.astype(jnp.float32).reshape(KSEL * BLK, HEADS, HDIM)) * score_scale
            fresh_part = soft_group(far_scores, None, far_values.reshape(KSEL * BLK, HEADS, HDIM), "qhk,khd->qhd")
            running = merge_parts(running, fresh_part)
        return (running[2] / running[1][..., None]).reshape(token_count, features).astype(jnp.bfloat16)

    stacked = lax.map(one_panel, jnp.arange(PANELS, dtype=jnp.int32))
    return stacked.reshape(SEQ, features)
```

```python
import jax
import jax.numpy as jnp
from jax import lax
from jax.sharding import PartitionSpec as P

HEADS = 16
BLK = 128
WIN = 4


def passed_along(block, axis, distance):
    devices = range(lax.axis_size(axis))
    route = [(i - distance, i) for i in devices if i - distance in devices]
    return lax.ppermute(block, axis, route)


def from_partner(value, axis, stride):
    mask = 2**stride
    pairs = [(source, source ^ mask) for source in range(lax.axis_size(axis))]
    return lax.ppermute(value, axis, pairs)


def window_visible(widths, first_block, block_len, window):
    row_count = widths.shape[0]
    offsets = jnp.arange(window * block_len, dtype=jnp.int32) // block_len
    key_pos = jnp.arange(window * block_len, dtype=jnp.int32) % block_len
    query_pos = jnp.arange(block_len, dtype=jnp.int32)
    block_ids = first_block + jnp.arange(row_count, dtype=jnp.int32)
    inside = offsets[None, None, :] < widths[:, None, None]
    started = block_ids[:, None, None] - offsets[None, None, :] >= 0
    causal = (offsets[None, None, :] > 0) | (key_pos[None, None, :] <= query_pos[None, :, None])
    return inside & started & causal


def pick_blocks(source, block_index):
    return lax.dynamic_slice_in_dim(source, block_index[0] * BLK, BLK, 0)


def on_device(queries, key_rows, value_rows, widths, columns):
    token_count, features = queries.shape
    panel_len = token_count // BLK
    head_dim = features // HEADS
    score_scale = head_dim ** (-0.5)
    device = lax.axis_index("outer")
    level_count = lax.axis_size("outer").bit_length() - 1
    rim_len = (WIN - 1) * BLK
    prev_keys, prev_values = passed_along((key_rows, value_rows), "outer", 1)
    ext_keys = jnp.concatenate([prev_keys, key_rows], axis=0)
    ext_values = jnp.concatenate([prev_values, value_rows], axis=0)

    def window_stack(extended):
        return jnp.concatenate(
            [
                extended[(WIN - 1 - offset) * BLK : (WIN - 1 - offset) * BLK + token_count].reshape(
                    panel_len, BLK, HEADS, head_dim
                )
                for offset in range(WIN)
            ],
            axis=1,
        )

    query_four = queries.reshape(panel_len, BLK, HEADS, head_dim)
    scores = (
        jnp.einsum(
            "pqhd,pkhd->pqhk",
            query_four,
            window_stack(ext_keys),
            preferred_element_type=jnp.float32,
        )
        * score_scale
    )
    visible = window_visible(widths, device * panel_len, BLK, WIN)
    masked = jnp.where(visible[:, :, None, :], scores, -jnp.inf)
    win_max = jnp.max(masked, axis=-1)
    win_weights = jnp.exp(masked - win_max[..., None])
    win_total = jnp.sum(win_weights, axis=-1)
    win_sum = jnp.einsum(
        "pqhk,pkhd->pqhd",
        win_weights.astype(jnp.bfloat16),
        window_stack(ext_values),
        preferred_element_type=jnp.float32,
    )
    win_max = win_max.reshape(token_count, HEADS)
    win_total = win_total.reshape(token_count, HEADS)
    win_sum = win_sum.reshape(token_count, HEADS, head_dim)
    bit_order = list(range(level_count))
    key_list = [None] * level_count
    value_list = [None] * level_count
    for level_bit in bit_order:
        partner = jnp.bitwise_xor(device, 1 << level_bit)
        wanted = columns[partner, level_bit] - device * panel_len
        far_keys, far_values = from_partner(
            (pick_blocks(key_rows, wanted), pick_blocks(value_rows, wanted)), "outer", level_bit
        )
        key_list[level_bit] = far_keys
        value_list[level_bit] = far_values
    far_count = key_list[0].shape[0]
    all_keys = jnp.stack(key_list, axis=0).reshape(level_count, far_count, HEADS, head_dim)
    all_values = jnp.stack(value_list, axis=0).reshape(level_count, far_count, HEADS, head_dim)
    query_three = queries.reshape(token_count, HEADS, head_dim)
    far_scores = (
        jnp.einsum("qhd,lkhd->qhlk", query_three, all_keys, preferred_element_type=jnp.float32)
        * score_scale
    )
    far_max = jnp.max(far_scores, axis=-1)
    far_weights = jnp.exp(far_scores - far_max[..., None])
    far_total = jnp.sum(far_weights, axis=-1)
    far_sum = jnp.einsum(
        "qhlk,lkhd->qhld",
        far_weights.astype(jnp.bfloat16),
        all_values,
        preferred_element_type=jnp.float32,
    )
    top_max = jnp.maximum(win_max, jnp.max(far_max, axis=-1))
    win_factor = jnp.exp(win_max - top_max)
    far_factor = jnp.exp(far_max - top_max[..., None])
    total = win_total * win_factor + jnp.sum(far_total * far_factor, axis=-1)
    output = win_sum * win_factor[..., None] + jnp.sum(far_sum * far_factor[..., None], axis=2)
    context = output / total[..., None]
    return context.reshape(token_count, features).astype(jnp.bfloat16)


def solution(mesh):
    placed = (
        P(("groups", "outer"), None),
        P(("groups", "outer"), None),
        P(("groups", "outer"), None),
        P(("groups", "outer")),
        P("groups", None, None),
    )
    return jax.shard_map(
        on_device,
        mesh=mesh,
        in_specs=placed,
        out_specs=P(("groups", "outer"), None),
        check_vma=False,
    )
```

```python
import functools

import jax
import jax.numpy as jnp
from jax import lax
from jax.experimental import pallas as pl
from jax.experimental.pallas import tpu as pltpu
from jax.sharding import PartitionSpec as P

HEADS = 16
BLK = 128
WIN = 4


def passed_along(block, axis, distance):
    devices = range(lax.axis_size(axis))
    route = [(i - distance, i) for i in devices if i - distance in devices]
    return lax.ppermute(block, axis, route)


def from_partner(value, axis, stride):
    mask = 2**stride
    pairs = [(source, source ^ mask) for source in range(lax.axis_size(axis))]
    return lax.ppermute(value, axis, pairs)


def pick_blocks(source, block_index):
    return lax.dynamic_slice_in_dim(source, block_index[0] * BLK, BLK, 0)


def _nt(a, b):
    return lax.dot_general(a, b, (((1,), (1,)), ((), ())), preferred_element_type=jnp.float32)


def _nn(a, b):
    return lax.dot_general(a, b, (((1,), (0,)), ((), ())), preferred_element_type=jnp.float32)


def attend_kernel(level_count, meta, q_ref, ok_ref, ov_ref, pk_ref, pv_ref, *rest):
    far_refs = rest[: 2 * level_count]
    out_ref = rest[2 * level_count]
    rows, head_dim = q_ref.shape
    panel_len = rows // BLK
    scale = head_dim ** (-0.5)
    q = q_ref[...]

    row = lax.broadcasted_iota(jnp.int32, (rows, rows), 0)
    col = lax.broadcasted_iota(jnp.int32, (rows, rows), 1)
    q_blk = row // BLK
    k_blk = col // BLK
    width = jnp.zeros((rows, rows), jnp.int32)
    for r in range(panel_len):
        width = jnp.where(q_blk == r, meta[r], width)
    first_block = meta[panel_len]

    own_off = q_blk - k_blk
    own_vis = (own_off >= 0) & (own_off < width) & ((own_off > 0) | (col <= row))
    prev_off = q_blk + panel_len - k_blk
    prev_vis = (prev_off < width) & (first_block + q_blk - prev_off >= 0)

    s_own = jnp.where(own_vis, _nt(q, ok_ref[...]) * scale, -jnp.inf)
    s_prev = jnp.where(prev_vis, _nt(q, pk_ref[...]) * scale, -jnp.inf)
    m_w = jnp.maximum(s_own.max(-1, keepdims=True), s_prev.max(-1, keepdims=True))
    e_own = jnp.exp(s_own - m_w)
    e_prev = jnp.exp(s_prev - m_w)
    l_w = e_own.sum(-1, keepdims=True) + e_prev.sum(-1, keepdims=True)
    o_w = _nn(e_own.astype(jnp.bfloat16), ov_ref[...]) + _nn(e_prev.astype(jnp.bfloat16), pv_ref[...])

    maxes, totals, sums = [m_w], [l_w], [o_w]
    for b in range(level_count):
        s = _nt(q, far_refs[2 * b][...]) * scale
        m = s.max(-1, keepdims=True)
        e = jnp.exp(s - m)
        maxes.append(m)
        totals.append(e.sum(-1, keepdims=True))
        sums.append(_nn(e.astype(jnp.bfloat16), far_refs[2 * b + 1][...]))

    top = maxes[0]
    for m in maxes[1:]:
        top = jnp.maximum(top, m)
    total = jnp.zeros_like(l_w)
    output = jnp.zeros_like(o_w)
    for m, l, o in zip(maxes, totals, sums):
        factor = jnp.exp(m - top)
        total = total + l * factor
        output = output + o * factor
    out_ref[...] = (output / total).astype(out_ref.dtype)


def attend(meta, queries, own_k, own_v, prev_k, prev_v, far):
    rows, features = queries.shape
    head_dim = features // HEADS
    level_count = len(far)
    far_rows = far[0].shape[0] // 2
    panel = pl.BlockSpec((rows, head_dim), lambda h, meta: (0, h))
    far_specs = []
    for _ in range(level_count):
        far_specs.append(pl.BlockSpec((far_rows, head_dim), lambda h, meta: (0, h)))
        far_specs.append(pl.BlockSpec((far_rows, head_dim), lambda h, meta: (1, h)))
    far_args = []
    for block in far:
        far_args += [block, block]
    keys = 2 * rows + level_count * far_rows
    flops = 4 * rows * keys * features
    return pl.pallas_call(
        functools.partial(attend_kernel, level_count),
        out_shape=jax.ShapeDtypeStruct((rows, features), queries.dtype),
        grid_spec=pltpu.PrefetchScalarGridSpec(
            num_scalar_prefetch=1,
            grid=(HEADS,),
            in_specs=[panel] * 5 + far_specs,
            out_specs=panel,
        ),
        compiler_params=pltpu.CompilerParams(dimension_semantics=("arbitrary",)),
        cost_estimate=pl.CostEstimate(
            flops=flops,
            transcendentals=rows * keys * HEADS,
            bytes_accessed=2 * features * (6 * rows + 2 * level_count * far_rows),
        ),
    )(meta, queries, own_k, own_v, prev_k, prev_v, *far_args)


def on_device(queries, key_rows, value_rows, widths, columns):
    token_count, features = queries.shape
    panel_len = token_count // BLK
    device = lax.axis_index("outer")
    level_count = lax.axis_size("outer").bit_length() - 1
    prev_keys, prev_values = passed_along((key_rows, value_rows), "outer", 1)
    far = []
    for level_bit in range(level_count):
        partner = jnp.bitwise_xor(device, 1 << level_bit)
        wanted = columns[partner, level_bit] - device * panel_len
        outgoing = jnp.concatenate([pick_blocks(key_rows, wanted), pick_blocks(value_rows, wanted)], axis=0)
        far.append(from_partner(outgoing, "outer", level_bit))
    meta = jnp.concatenate([widths, (device * panel_len)[None]]).astype(jnp.int32)
    return attend(meta, queries, key_rows, value_rows, prev_keys, prev_values, far)


def solution(mesh):
    placed = (
        P(("groups", "outer"), None),
        P(("groups", "outer"), None),
        P(("groups", "outer"), None),
        P(("groups", "outer")),
        P("groups", None, None),
    )
    return jax.shard_map(
        on_device,
        mesh=mesh,
        in_specs=placed,
        out_specs=P(("groups", "outer"), None),
        check_vma=False,
    )
```

```python
import functools

import jax
import jax.numpy as jnp
from jax import lax
from jax.experimental import pallas as pl
from jax.experimental.pallas import tpu as pltpu
from jax.sharding import PartitionSpec as P

HEADS = 16
BLK = 128
WIN = 4


def passed_along(block, axis, distance):
    devices = range(lax.axis_size(axis))
    route = [(i - distance, i) for i in devices if i - distance in devices]
    return lax.ppermute(block, axis, route)


def from_partner(value, axis, stride):
    mask = 2**stride
    pairs = [(source, source ^ mask) for source in range(lax.axis_size(axis))]
    return lax.ppermute(value, axis, pairs)


def pick_blocks(source, block_index):
    return lax.dynamic_slice_in_dim(source, block_index[0] * BLK, BLK, 0)


def _nt(a, b):
    return lax.dot_general(a, b, (((1,), (1,)), ((), ())), preferred_element_type=jnp.float32)


def _nn(a, b):
    return lax.dot_general(a, b, (((1,), (0,)), ((), ())), preferred_element_type=jnp.float32)


def attend_kernel(level_count, meta, q_ref, ok_ref, ov_ref, pk_ref, pv_ref, *rest):
    far_refs = rest[: 2 * level_count]
    out_ref = rest[2 * level_count]
    bias_ref = rest[2 * level_count + 1]
    rows, head_dim = q_ref.shape
    panel_len = rows // BLK
    scale = head_dim ** (-0.5)
    span = WIN * BLK

    @pl.when(pl.program_id(0) == 0)
    def _():
        query = lax.broadcasted_iota(jnp.int32, (BLK, span), 0)
        column = lax.broadcasted_iota(jnp.int32, (BLK, span), 1)
        first_block = meta[panel_len]
        for r in range(panel_len):
            width = meta[r]
            split = (panel_len - r) * BLK
            key_block = jnp.where(column < split, column // BLK + r - panel_len, (column - split) // BLK)
            offset = r - key_block
            visible = (offset < width) & (first_block + key_block >= 0) & ((offset > 0) | (column % BLK <= query))
            bias_ref[r * BLK : (r + 1) * BLK, :] = jnp.where(visible, 0.0, -jnp.inf)

    for r in range(panel_len):
        rows_r = slice(r * BLK, (r + 1) * BLK)
        split = (panel_len - r) * BLK
        q = q_ref[rows_r, :]
        bias = bias_ref[rows_r, :]
        s_prev = _nt(q, pk_ref[r * BLK :, :]) * scale + bias[:, :split]
        s_own = _nt(q, ok_ref[: (r + 1) * BLK, :]) * scale + bias[:, split:]
        m_w = jnp.maximum(s_own.max(-1, keepdims=True), s_prev.max(-1, keepdims=True))
        e_own = jnp.exp(s_own - m_w)
        e_prev = jnp.exp(s_prev - m_w)
        l_w = e_own.sum(-1, keepdims=True) + e_prev.sum(-1, keepdims=True)
        o_w = _nn(e_own.astype(jnp.bfloat16), ov_ref[: (r + 1) * BLK, :]) + _nn(
            e_prev.astype(jnp.bfloat16), pv_ref[r * BLK :, :]
        )
        maxes, totals, sums = [m_w], [l_w], [o_w]
        for b in range(level_count):
            s = _nt(q, far_refs[2 * b][...]) * scale
            m = s.max(-1, keepdims=True)
            e = jnp.exp(s - m)
            maxes.append(m)
            totals.append(e.sum(-1, keepdims=True))
            sums.append(_nn(e.astype(jnp.bfloat16), far_refs[2 * b + 1][...]))
        top = maxes[0]
        for m in maxes[1:]:
            top = jnp.maximum(top, m)
        total = jnp.zeros_like(l_w)
        output = jnp.zeros_like(o_w)
        for m, l, o in zip(maxes, totals, sums):
            factor = jnp.exp(m - top)
            total = total + l * factor
            output = output + o * factor
        out_ref[rows_r, :] = (output / total).astype(out_ref.dtype)


def attend(meta, queries, own_k, own_v, prev_k, prev_v, far):
    rows, features = queries.shape
    head_dim = features // HEADS
    level_count = len(far)
    far_rows = far[0].shape[0] // 2
    panel = pl.BlockSpec((rows, head_dim), lambda h, meta: (0, h))
    far_specs = []
    for _ in range(level_count):
        far_specs.append(pl.BlockSpec((far_rows, head_dim), lambda h, meta: (0, h)))
        far_specs.append(pl.BlockSpec((far_rows, head_dim), lambda h, meta: (1, h)))
    far_args = []
    for block in far:
        far_args += [block, block]
    keys = WIN * BLK + level_count * far_rows
    flops = 4 * rows * keys * features
    return pl.pallas_call(
        functools.partial(attend_kernel, level_count),
        out_shape=jax.ShapeDtypeStruct((rows, features), queries.dtype),
        grid_spec=pltpu.PrefetchScalarGridSpec(
            num_scalar_prefetch=1,
            grid=(HEADS,),
            in_specs=[panel] * 5 + far_specs,
            out_specs=panel,
            scratch_shapes=[pltpu.VMEM((rows, WIN * BLK), jnp.float32)],
        ),
        compiler_params=pltpu.CompilerParams(dimension_semantics=("arbitrary",)),
        cost_estimate=pl.CostEstimate(
            flops=flops,
            transcendentals=rows * keys * HEADS,
            bytes_accessed=2 * features * (6 * rows + 2 * level_count * far_rows),
        ),
    )(meta, queries, own_k, own_v, prev_k, prev_v, *far_args)


def on_device(queries, key_rows, value_rows, widths, columns):
    token_count, features = queries.shape
    panel_len = token_count // BLK
    device = lax.axis_index("outer")
    level_count = lax.axis_size("outer").bit_length() - 1
    prev_keys, prev_values = passed_along((key_rows, value_rows), "outer", 1)
    far = []
    for level_bit in range(level_count):
        partner = jnp.bitwise_xor(device, 1 << level_bit)
        wanted = columns[partner, level_bit] - device * panel_len
        outgoing = jnp.concatenate([pick_blocks(key_rows, wanted), pick_blocks(value_rows, wanted)], axis=0)
        far.append(from_partner(outgoing, "outer", level_bit))
    meta = jnp.concatenate([widths, (device * panel_len)[None]]).astype(jnp.int32)
    return attend(meta, queries, key_rows, value_rows, prev_keys, prev_values, far)


def solution(mesh):
    placed = (
        P(("groups", "outer"), None),
        P(("groups", "outer"), None),
        P(("groups", "outer"), None),
        P(("groups", "outer")),
        P("groups", None, None),
    )
    return jax.shard_map(
        on_device,
        mesh=mesh,
        in_specs=placed,
        out_specs=P(("groups", "outer"), None),
        check_vma=False,
    )
```

```python
import functools

import jax
import jax.numpy as jnp
from jax import lax
from jax.experimental import pallas as pl
from jax.experimental.pallas import tpu as pltpu
from jax.sharding import PartitionSpec as P

HEADS = 16
BLK = 128
WIN = 4


def passed_along(block, axis, distance):
    devices = range(lax.axis_size(axis))
    route = [(i - distance, i) for i in devices if i - distance in devices]
    return lax.ppermute(block, axis, route)


def from_partner(value, axis, stride):
    mask = 2**stride
    pairs = [(source, source ^ mask) for source in range(lax.axis_size(axis))]
    return lax.ppermute(value, axis, pairs)


def pick_blocks(source, block_index):
    return lax.dynamic_slice_in_dim(source, block_index[0] * BLK, BLK, 0)


def _nt(a, b):
    return lax.dot_general(a, b, (((1,), (1,)), ((), ())), preferred_element_type=jnp.float32)


def _nn(a, b):
    return lax.dot_general(a, b, (((1,), (0,)), ((), ())), preferred_element_type=jnp.float32)


def attend_kernel(level_count, meta, q_ref, ok_ref, ov_ref, pk_ref, pv_ref, *rest):
    far_refs = rest[: 2 * level_count]
    out_ref = rest[2 * level_count]
    bias_ref = rest[2 * level_count + 1]
    rows, head_dim = q_ref.shape
    panel_len = rows // BLK
    scale = head_dim ** (-0.5)

    @pl.when(pl.program_id(0) == 0)
    def _():
        row = lax.broadcasted_iota(jnp.int32, (rows, rows), 0)
        col = lax.broadcasted_iota(jnp.int32, (rows, rows), 1)
        q_blk = row // BLK
        k_blk = col // BLK
        width = jnp.zeros((rows, rows), jnp.int32)
        for r in range(panel_len):
            width = jnp.where(q_blk == r, meta[r], width)
        first_block = meta[panel_len]
        own_off = q_blk - k_blk
        own_vis = (own_off >= 0) & (own_off < width) & ((own_off > 0) | (col <= row))
        prev_off = q_blk + panel_len - k_blk
        prev_vis = (prev_off < width) & (first_block + q_blk - prev_off >= 0)
        bias_ref[:, :rows] = jnp.where(prev_vis, 0.0, -jnp.inf)
        bias_ref[:, rows:] = jnp.where(own_vis, 0.0, -jnp.inf)

    q = q_ref[...]
    s_prev = _nt(q, pk_ref[...]) * scale + bias_ref[:, :rows]
    s_own = _nt(q, ok_ref[...]) * scale + bias_ref[:, rows:]
    m_w = jnp.maximum(s_own.max(-1, keepdims=True), s_prev.max(-1, keepdims=True))
    e_own = jnp.exp(s_own - m_w)
    e_prev = jnp.exp(s_prev - m_w)
    l_w = e_own.sum(-1, keepdims=True) + e_prev.sum(-1, keepdims=True)
    o_w = _nn(e_own.astype(jnp.bfloat16), ov_ref[...]) + _nn(e_prev.astype(jnp.bfloat16), pv_ref[...])

    maxes, totals, sums = [m_w], [l_w], [o_w]
    for b in range(level_count):
        s = _nt(q, far_refs[2 * b][...]) * scale
        m = s.max(-1, keepdims=True)
        e = jnp.exp(s - m)
        maxes.append(m)
        totals.append(e.sum(-1, keepdims=True))
        sums.append(_nn(e.astype(jnp.bfloat16), far_refs[2 * b + 1][...]))

    top = maxes[0]
    for m in maxes[1:]:
        top = jnp.maximum(top, m)
    total = jnp.zeros_like(l_w)
    output = jnp.zeros_like(o_w)
    for m, l, o in zip(maxes, totals, sums):
        factor = jnp.exp(m - top)
        total = total + l * factor
        output = output + o * factor
    out_ref[...] = (output / total).astype(out_ref.dtype)


def attend(meta, queries, own_k, own_v, prev_k, prev_v, far):
    rows, features = queries.shape
    head_dim = features // HEADS
    level_count = len(far)
    far_rows = far[0].shape[0] // 2
    panel = pl.BlockSpec((rows, head_dim), lambda h, meta: (0, h))
    far_specs = []
    for _ in range(level_count):
        far_specs.append(pl.BlockSpec((far_rows, head_dim), lambda h, meta: (0, h)))
        far_specs.append(pl.BlockSpec((far_rows, head_dim), lambda h, meta: (1, h)))
    far_args = []
    for block in far:
        far_args += [block, block]
    keys = 2 * rows + level_count * far_rows
    flops = 4 * rows * keys * features
    return pl.pallas_call(
        functools.partial(attend_kernel, level_count),
        out_shape=jax.ShapeDtypeStruct((rows, features), queries.dtype),
        grid_spec=pltpu.PrefetchScalarGridSpec(
            num_scalar_prefetch=1,
            grid=(HEADS,),
            in_specs=[panel] * 5 + far_specs,
            out_specs=panel,
            scratch_shapes=[pltpu.VMEM((rows, 2 * rows), jnp.float32)],
        ),
        compiler_params=pltpu.CompilerParams(dimension_semantics=("arbitrary",)),
        cost_estimate=pl.CostEstimate(
            flops=flops,
            transcendentals=rows * keys * HEADS,
            bytes_accessed=2 * features * (6 * rows + 2 * level_count * far_rows),
        ),
    )(meta, queries, own_k, own_v, prev_k, prev_v, *far_args)


def on_device(queries, key_rows, value_rows, widths, columns):
    token_count, features = queries.shape
    panel_len = token_count // BLK
    device = lax.axis_index("outer")
    level_count = lax.axis_size("outer").bit_length() - 1
    prev_keys, prev_values = passed_along((key_rows, value_rows), "outer", 1)
    far = []
    for level_bit in range(level_count):
        partner = jnp.bitwise_xor(device, 1 << level_bit)
        wanted = columns[partner, level_bit] - device * panel_len
        outgoing = jnp.concatenate([pick_blocks(key_rows, wanted), pick_blocks(value_rows, wanted)], axis=0)
        far.append(from_partner(outgoing, "outer", level_bit))
    meta = jnp.concatenate([widths, (device * panel_len)[None]]).astype(jnp.int32)
    return attend(meta, queries, key_rows, value_rows, prev_keys, prev_values, far)


def solution(mesh):
    placed = (
        P(("groups", "outer"), None),
        P(("groups", "outer"), None),
        P(("groups", "outer"), None),
        P(("groups", "outer")),
        P("groups", None, None),
    )
    return jax.shard_map(
        on_device,
        mesh=mesh,
        in_specs=placed,
        out_specs=P(("groups", "outer"), None),
        check_vma=False,
    )
```

```python
import functools

import jax
import jax.numpy as jnp
from jax import lax
from jax.experimental import pallas as pl
from jax.experimental.pallas import tpu as pltpu
from jax.sharding import PartitionSpec as P

HEADS = 16
BLK = 128
WIN = 4


def passed_along(block, axis, distance):
    devices = range(lax.axis_size(axis))
    route = [(i - distance, i) for i in devices if i - distance in devices]
    return lax.ppermute(block, axis, route)


def from_partner(value, axis, stride):
    mask = 2**stride
    pairs = [(source, source ^ mask) for source in range(lax.axis_size(axis))]
    return lax.ppermute(value, axis, pairs)


def pick_blocks(source, block_index):
    return lax.dynamic_slice_in_dim(source, block_index[0] * BLK, BLK, 0)


def _nt(a, b):
    return lax.dot_general(a, b, (((1,), (1,)), ((), ())), preferred_element_type=jnp.float32)


def _nn(a, b):
    return lax.dot_general(a, b, (((1,), (0,)), ((), ())), preferred_element_type=jnp.float32)


def levels_kernel(level_count, q_ref, *rest):
    far_refs = rest[: 2 * level_count]
    sum_ref, stat_ref = rest[2 * level_count :]
    head_dim = q_ref.shape[1]
    scale = head_dim ** (-0.5)
    q = q_ref[...]
    maxes, totals, sums = [], [], []
    for b in range(level_count):
        s = _nt(q, far_refs[2 * b][...]) * scale
        m = s.max(-1, keepdims=True)
        e = jnp.exp(s - m)
        maxes.append(m)
        totals.append(e.sum(-1, keepdims=True))
        sums.append(_nn(e.astype(jnp.bfloat16), far_refs[2 * b + 1][...]))
    top = maxes[0]
    for m in maxes[1:]:
        top = jnp.maximum(top, m)
    total = jnp.zeros_like(totals[0])
    output = jnp.zeros_like(sums[0])
    for m, l, o in zip(maxes, totals, sums):
        factor = jnp.exp(m - top)
        total = total + l * factor
        output = output + o * factor
    sum_ref[...] = output
    lane = lax.broadcasted_iota(jnp.int32, stat_ref.shape, 1)
    stat_ref[...] = jnp.where(lane < head_dim // 2, top, total)


def window_kernel(meta, q_ref, ok_ref, ov_ref, pk_ref, pv_ref, sum_ref, stat_ref, out_ref, bias_ref):
    rows, head_dim = q_ref.shape
    panel_len = rows // BLK
    scale = head_dim ** (-0.5)

    @pl.when(pl.program_id(0) == 0)
    def _():
        row = lax.broadcasted_iota(jnp.int32, (rows, rows), 0)
        col = lax.broadcasted_iota(jnp.int32, (rows, rows), 1)
        q_blk = row // BLK
        k_blk = col // BLK
        width = jnp.zeros((rows, rows), jnp.int32)
        for r in range(panel_len):
            width = jnp.where(q_blk == r, meta[r], width)
        first_block = meta[panel_len]
        own_off = q_blk - k_blk
        own_vis = (own_off >= 0) & (own_off < width) & ((own_off > 0) | (col <= row))
        prev_off = q_blk + panel_len - k_blk
        prev_vis = (prev_off < width) & (first_block + q_blk - prev_off >= 0)
        bias_ref[:, :rows] = jnp.where(prev_vis, 0.0, -jnp.inf)
        bias_ref[:, rows:] = jnp.where(own_vis, 0.0, -jnp.inf)

    q = q_ref[...]
    s_prev = _nt(q, pk_ref[...]) * scale + bias_ref[:, :rows]
    s_own = _nt(q, ok_ref[...]) * scale + bias_ref[:, rows:]
    m_w = jnp.maximum(s_own.max(-1, keepdims=True), s_prev.max(-1, keepdims=True))
    e_own = jnp.exp(s_own - m_w)
    e_prev = jnp.exp(s_prev - m_w)
    l_w = e_own.sum(-1, keepdims=True) + e_prev.sum(-1, keepdims=True)
    o_w = _nn(e_own.astype(jnp.bfloat16), ov_ref[...]) + _nn(e_prev.astype(jnp.bfloat16), pv_ref[...])

    m_f = stat_ref[:, :1]
    l_f = stat_ref[:, head_dim // 2 : head_dim // 2 + 1]
    top = jnp.maximum(m_w, m_f)
    w_factor = jnp.exp(m_w - top)
    f_factor = jnp.exp(m_f - top)
    total = l_w * w_factor + l_f * f_factor
    output = o_w * w_factor + sum_ref[...] * f_factor
    out_ref[...] = (output / total).astype(out_ref.dtype)


def far_levels(queries, far):
    rows, features = queries.shape
    head_dim = features // HEADS
    level_count = len(far)
    far_rows = far[0].shape[0] // 2
    panel = pl.BlockSpec((rows, head_dim), lambda h: (0, h))
    far_specs, far_args = [], []
    for block in far:
        far_specs.append(pl.BlockSpec((far_rows, head_dim), lambda h: (0, h)))
        far_specs.append(pl.BlockSpec((far_rows, head_dim), lambda h: (1, h)))
        far_args += [block, block]
    keys = level_count * far_rows
    return pl.pallas_call(
        functools.partial(levels_kernel, level_count),
        out_shape=(
            jax.ShapeDtypeStruct((rows, features), jnp.float32),
            jax.ShapeDtypeStruct((rows, features), jnp.float32),
        ),
        grid=(HEADS,),
        in_specs=[panel] + far_specs,
        out_specs=(panel, panel),
        compiler_params=pltpu.CompilerParams(dimension_semantics=("arbitrary",)),
        cost_estimate=pl.CostEstimate(
            flops=4 * rows * keys * features,
            transcendentals=rows * keys * HEADS,
            bytes_accessed=2 * features * (rows + 2 * keys) + 8 * rows * features,
        ),
    )(queries, *far_args)


def window(meta, queries, own_k, own_v, prev_k, prev_v, far_sum, far_stat):
    rows, features = queries.shape
    head_dim = features // HEADS
    panel = pl.BlockSpec((rows, head_dim), lambda h, meta: (0, h))
    return pl.pallas_call(
        window_kernel,
        out_shape=jax.ShapeDtypeStruct((rows, features), queries.dtype),
        grid_spec=pltpu.PrefetchScalarGridSpec(
            num_scalar_prefetch=1,
            grid=(HEADS,),
            in_specs=[panel] * 7,
            out_specs=panel,
            scratch_shapes=[pltpu.VMEM((rows, 2 * rows), jnp.float32)],
        ),
        compiler_params=pltpu.CompilerParams(dimension_semantics=("arbitrary",)),
        cost_estimate=pl.CostEstimate(
            flops=8 * rows * rows * features,
            transcendentals=2 * rows * rows * HEADS,
            bytes_accessed=12 * rows * features + 8 * rows * features,
        ),
    )(meta, queries, own_k, own_v, prev_k, prev_v, far_sum, far_stat)


def on_device(queries, key_rows, value_rows, widths, columns):
    token_count, features = queries.shape
    panel_len = token_count // BLK
    device = lax.axis_index("outer")
    level_count = lax.axis_size("outer").bit_length() - 1
    far = []
    for level_bit in range(level_count):
        partner = jnp.bitwise_xor(device, 1 << level_bit)
        wanted = columns[partner, level_bit] - device * panel_len
        outgoing = jnp.concatenate([pick_blocks(key_rows, wanted), pick_blocks(value_rows, wanted)], axis=0)
        far.append(from_partner(outgoing, "outer", level_bit))
    gate = far[1 : min(3, level_count)]
    rim_keys, rim_values, *_ = lax.optimization_barrier((key_rows, value_rows, *gate))
    prev_keys, prev_values = passed_along((rim_keys, rim_values), "outer", 1)
    far_sum, far_stat = far_levels(queries, far)
    meta = jnp.concatenate([widths, (device * panel_len)[None]]).astype(jnp.int32)
    return window(meta, queries, key_rows, value_rows, prev_keys, prev_values, far_sum, far_stat)


def solution(mesh):
    placed = (
        P(("groups", "outer"), None),
        P(("groups", "outer"), None),
        P(("groups", "outer"), None),
        P(("groups", "outer")),
        P("groups", None, None),
    )
    return jax.shard_map(
        on_device,
        mesh=mesh,
        in_specs=placed,
        out_specs=P(("groups", "outer"), None),
        check_vma=False,
    )
```

```python
import functools

import jax
import jax.numpy as jnp
from jax import lax
from jax.experimental import pallas as pl
from jax.experimental.pallas import tpu as pltpu
from jax.sharding import PartitionSpec as P

HEADS = 16
BLK = 128
WIN = 4
CHUNKS = 2


def passed_along(block, axis, distance):
    devices = range(lax.axis_size(axis))
    route = [(i - distance, i) for i in devices if i - distance in devices]
    return lax.ppermute(block, axis, route)


def from_partner(value, axis, stride):
    mask = 2**stride
    pairs = [(source, source ^ mask) for source in range(lax.axis_size(axis))]
    return lax.ppermute(value, axis, pairs)


def pick_blocks(source, block_index):
    return lax.dynamic_slice_in_dim(source, block_index[0] * BLK, BLK, 0)


def _nt(a, b):
    return lax.dot_general(a, b, (((1,), (1,)), ((), ())), preferred_element_type=jnp.float32)


def _nn(a, b):
    return lax.dot_general(a, b, (((1,), (0,)), ((), ())), preferred_element_type=jnp.float32)


def attend_kernel(level_count, meta, q_ref, ok_ref, ov_ref, pk_ref, pv_ref, *rest):
    far_refs = rest[: 2 * level_count]
    out_ref, bias_ref = rest[-2:]
    rows, head_dim = q_ref.shape
    panel_len = rows // BLK
    scale = head_dim ** (-0.5)

    @pl.when(pl.program_id(0) == 0)
    def _():
        row = lax.broadcasted_iota(jnp.int32, (rows, rows), 0)
        col = lax.broadcasted_iota(jnp.int32, (rows, rows), 1)
        q_blk = row // BLK
        k_blk = col // BLK
        width = jnp.zeros((rows, rows), jnp.int32)
        for r in range(panel_len):
            width = jnp.where(q_blk == r, meta[r], width)
        first_block = meta[panel_len]
        own_off = q_blk - k_blk
        own_vis = (own_off >= 0) & (own_off < width) & ((own_off > 0) | (col <= row))
        prev_off = q_blk + panel_len - k_blk
        prev_vis = (prev_off < width) & (first_block + q_blk - prev_off >= 0)
        bias_ref[:, :rows] = jnp.where(prev_vis, 0.0, -jnp.inf)
        bias_ref[:, rows:] = jnp.where(own_vis, 0.0, -jnp.inf)

    q = q_ref[...]
    s_prev = _nt(q, pk_ref[...]) * scale + bias_ref[:, :rows]
    s_own = _nt(q, ok_ref[...]) * scale + bias_ref[:, rows:]
    m_w = jnp.maximum(s_own.max(-1, keepdims=True), s_prev.max(-1, keepdims=True))
    e_own = jnp.exp(s_own - m_w)
    e_prev = jnp.exp(s_prev - m_w)
    l_w = e_own.sum(-1, keepdims=True) + e_prev.sum(-1, keepdims=True)
    o_w = _nn(e_own.astype(jnp.bfloat16), ov_ref[...]) + _nn(e_prev.astype(jnp.bfloat16), pv_ref[...])

    maxes, totals, sums = [m_w], [l_w], [o_w]
    for b in range(level_count):
        s = _nt(q, far_refs[2 * b][...]) * scale
        m = s.max(-1, keepdims=True)
        e = jnp.exp(s - m)
        maxes.append(m)
        totals.append(e.sum(-1, keepdims=True))
        sums.append(_nn(e.astype(jnp.bfloat16), far_refs[2 * b + 1][...]))

    top = maxes[0]
    for m in maxes[1:]:
        top = jnp.maximum(top, m)
    total = jnp.zeros_like(l_w)
    output = jnp.zeros_like(o_w)
    for m, l, o in zip(maxes, totals, sums):
        factor = jnp.exp(m - top)
        total = total + l * factor
        output = output + o * factor
    out_ref[...] = (output / total).astype(out_ref.dtype)


def attend(meta, queries, own_k, own_v, prev_k, prev_v, far, first_head, prior=None):
    rows, features = queries.shape
    head_dim = features // HEADS
    heads = prev_k.shape[1] // head_dim
    level_count = len(far)
    far_rows = far[0].shape[0] // 2
    whole = pl.BlockSpec((rows, head_dim), lambda h, meta: (0, h + first_head))
    part = pl.BlockSpec((rows, head_dim), lambda h, meta: (0, h))
    far_specs = []
    for _ in range(level_count):
        far_specs.append(pl.BlockSpec((far_rows, head_dim), lambda h, meta: (0, h)))
        far_specs.append(pl.BlockSpec((far_rows, head_dim), lambda h, meta: (1, h)))
    far_args = []
    for block in far:
        far_args += [block, block]
    keys = 2 * rows + level_count * far_rows
    args = [meta, queries, own_k, own_v, prev_k, prev_v, *far_args]
    in_specs = [whole] * 3 + [part] * 2 + far_specs
    aliases = {}
    if prior is not None:
        aliases = {len(args): 0}
        args.append(prior)
        in_specs.append(pl.BlockSpec(memory_space=pl.ANY))
    return pl.pallas_call(
        functools.partial(attend_kernel, level_count),
        out_shape=jax.ShapeDtypeStruct((rows, features), queries.dtype),
        grid_spec=pltpu.PrefetchScalarGridSpec(
            num_scalar_prefetch=1,
            grid=(heads,),
            in_specs=in_specs,
            out_specs=whole,
            scratch_shapes=[pltpu.VMEM((rows, 2 * rows), jnp.float32)],
        ),
        input_output_aliases=aliases,
        compiler_params=pltpu.CompilerParams(dimension_semantics=("arbitrary",)),
        cost_estimate=pl.CostEstimate(
            flops=4 * rows * keys * head_dim * heads,
            transcendentals=rows * keys * heads,
            bytes_accessed=2 * head_dim * heads * (6 * rows + 2 * level_count * far_rows),
        ),
    )(*args)


def on_device(queries, key_rows, value_rows, widths, columns):
    token_count, features = queries.shape
    panel_len = token_count // BLK
    device = lax.axis_index("outer")
    level_count = lax.axis_size("outer").bit_length() - 1
    meta = jnp.concatenate([widths, (device * panel_len)[None]]).astype(jnp.int32)
    wanted = [columns[jnp.bitwise_xor(device, 1 << b), b] - device * panel_len for b in range(level_count)]
    width = features // CHUNKS
    context = None
    for c in range(CHUNKS):
        cols = slice(c * width, (c + 1) * width)
        prev_keys, prev_values = passed_along((key_rows[:, cols], value_rows[:, cols]), "outer", 1)
        far = []
        for level_bit in range(level_count):
            outgoing = jnp.concatenate(
                [pick_blocks(key_rows, wanted[level_bit])[:, cols], pick_blocks(value_rows, wanted[level_bit])[:, cols]],
                axis=0,
            )
            far.append(from_partner(outgoing, "outer", level_bit))
        context = attend(
            meta, queries, key_rows, value_rows, prev_keys, prev_values, far, c * (HEADS // CHUNKS), context
        )
    return context


def solution(mesh):
    placed = (
        P(("groups", "outer"), None),
        P(("groups", "outer"), None),
        P(("groups", "outer"), None),
        P(("groups", "outer")),
        P("groups", None, None),
    )
    return jax.shard_map(
        on_device,
        mesh=mesh,
        in_specs=placed,
        out_specs=P(("groups", "outer"), None),
        check_vma=False,
    )
```

```python
import functools

import jax
import jax.numpy as jnp
from jax import lax
from jax.experimental import pallas as pl
from jax.experimental.pallas import tpu as pltpu
from jax.sharding import PartitionSpec as P

HEADS = 16
BLK = 128
WIN = 4
CHUNKS = 4


def passed_along(block, axis, distance):
    devices = range(lax.axis_size(axis))
    route = [(i - distance, i) for i in devices if i - distance in devices]
    return lax.ppermute(block, axis, route)


def from_partner(value, axis, stride):
    mask = 2**stride
    pairs = [(source, source ^ mask) for source in range(lax.axis_size(axis))]
    return lax.ppermute(value, axis, pairs)


def pick_blocks(source, block_index):
    return lax.dynamic_slice_in_dim(source, block_index[0] * BLK, BLK, 0)


def _nt(a, b):
    return lax.dot_general(a, b, (((1,), (1,)), ((), ())), preferred_element_type=jnp.float32)


def _nn(a, b):
    return lax.dot_general(a, b, (((1,), (0,)), ((), ())), preferred_element_type=jnp.float32)


def attend_kernel(level_count, meta, q_ref, ok_ref, ov_ref, pk_ref, pv_ref, *rest):
    far_refs = rest[: 2 * level_count]
    out_ref, bias_ref = rest[-2:]
    rows, head_dim = q_ref.shape
    panel_len = rows // BLK
    scale = head_dim ** (-0.5)

    @pl.when(pl.program_id(0) == 0)
    def _():
        row = lax.broadcasted_iota(jnp.int32, (rows, rows), 0)
        col = lax.broadcasted_iota(jnp.int32, (rows, rows), 1)
        q_blk = row // BLK
        k_blk = col // BLK
        width = jnp.zeros((rows, rows), jnp.int32)
        for r in range(panel_len):
            width = jnp.where(q_blk == r, meta[r], width)
        first_block = meta[panel_len]
        own_off = q_blk - k_blk
        own_vis = (own_off >= 0) & (own_off < width) & ((own_off > 0) | (col <= row))
        prev_off = q_blk + panel_len - k_blk
        prev_vis = (prev_off < width) & (first_block + q_blk - prev_off >= 0)
        bias_ref[:, :rows] = jnp.where(prev_vis, 0.0, -jnp.inf)
        bias_ref[:, rows:] = jnp.where(own_vis, 0.0, -jnp.inf)

    q = q_ref[...]
    s_prev = _nt(q, pk_ref[...]) * scale + bias_ref[:, :rows]
    s_own = _nt(q, ok_ref[...]) * scale + bias_ref[:, rows:]
    m_w = jnp.maximum(s_own.max(-1, keepdims=True), s_prev.max(-1, keepdims=True))
    e_own = jnp.exp(s_own - m_w)
    e_prev = jnp.exp(s_prev - m_w)
    l_w = e_own.sum(-1, keepdims=True) + e_prev.sum(-1, keepdims=True)
    o_w = _nn(e_own.astype(jnp.bfloat16), ov_ref[...]) + _nn(e_prev.astype(jnp.bfloat16), pv_ref[...])

    maxes, totals, sums = [m_w], [l_w], [o_w]
    for b in range(level_count):
        s = _nt(q, far_refs[2 * b][...]) * scale
        m = s.max(-1, keepdims=True)
        e = jnp.exp(s - m)
        maxes.append(m)
        totals.append(e.sum(-1, keepdims=True))
        sums.append(_nn(e.astype(jnp.bfloat16), far_refs[2 * b + 1][...]))

    top = maxes[0]
    for m in maxes[1:]:
        top = jnp.maximum(top, m)
    total = jnp.zeros_like(l_w)
    output = jnp.zeros_like(o_w)
    for m, l, o in zip(maxes, totals, sums):
        factor = jnp.exp(m - top)
        total = total + l * factor
        output = output + o * factor
    out_ref[...] = (output / total).astype(out_ref.dtype)


def attend(meta, queries, own_k, own_v, rim, far, first_head, prior=None):
    rows, features = queries.shape
    head_dim = features // HEADS
    heads = rim.shape[1] // head_dim
    level_count = len(far)
    far_rows = far[0].shape[0] // 2
    whole = pl.BlockSpec((rows, head_dim), lambda h, meta: (0, h + first_head))
    rim_k = pl.BlockSpec((rows, head_dim), lambda h, meta: (0, h))
    rim_v = pl.BlockSpec((rows, head_dim), lambda h, meta: (1, h))
    far_specs = []
    for _ in range(level_count):
        far_specs.append(pl.BlockSpec((far_rows, head_dim), lambda h, meta: (0, h)))
        far_specs.append(pl.BlockSpec((far_rows, head_dim), lambda h, meta: (1, h)))
    far_args = []
    for block in far:
        far_args += [block, block]
    keys = 2 * rows + level_count * far_rows
    args = [meta, queries, own_k, own_v, rim, rim, *far_args]
    in_specs = [whole] * 3 + [rim_k, rim_v] + far_specs
    aliases = {}
    if prior is not None:
        aliases = {len(args): 0}
        args.append(prior)
        in_specs.append(pl.BlockSpec(memory_space=pl.ANY))
    return pl.pallas_call(
        functools.partial(attend_kernel, level_count),
        out_shape=jax.ShapeDtypeStruct((rows, features), queries.dtype),
        grid_spec=pltpu.PrefetchScalarGridSpec(
            num_scalar_prefetch=1,
            grid=(heads,),
            in_specs=in_specs,
            out_specs=whole,
            scratch_shapes=[pltpu.VMEM((rows, 2 * rows), jnp.float32)],
        ),
        input_output_aliases=aliases,
        compiler_params=pltpu.CompilerParams(dimension_semantics=("arbitrary",)),
        cost_estimate=pl.CostEstimate(
            flops=4 * rows * keys * head_dim * heads,
            transcendentals=rows * keys * heads,
            bytes_accessed=2 * head_dim * heads * (6 * rows + 2 * level_count * far_rows),
        ),
    )(*args)


def on_device(queries, key_rows, value_rows, widths, columns):
    token_count, features = queries.shape
    panel_len = token_count // BLK
    device = lax.axis_index("outer")
    level_count = lax.axis_size("outer").bit_length() - 1
    meta = jnp.concatenate([widths, (device * panel_len)[None]]).astype(jnp.int32)
    wanted = [columns[jnp.bitwise_xor(device, 1 << b), b] - device * panel_len for b in range(level_count)]
    width = features // CHUNKS
    context = None
    for c in range(CHUNKS):
        cols = slice(c * width, (c + 1) * width)
        rim = passed_along(jnp.concatenate([key_rows[:, cols], value_rows[:, cols]], axis=0), "outer", 1)
        far = []
        for level_bit in range(level_count):
            outgoing = jnp.concatenate(
                [pick_blocks(key_rows, wanted[level_bit])[:, cols], pick_blocks(value_rows, wanted[level_bit])[:, cols]],
                axis=0,
            )
            far.append(from_partner(outgoing, "outer", level_bit))
        context = attend(
            meta, queries, key_rows, value_rows, rim, far, c * (HEADS // CHUNKS), context
        )
    return context


def solution(mesh):
    placed = (
        P(("groups", "outer"), None),
        P(("groups", "outer"), None),
        P(("groups", "outer"), None),
        P(("groups", "outer")),
        P("groups", None, None),
    )
    return jax.shard_map(
        on_device,
        mesh=mesh,
        in_specs=placed,
        out_specs=P(("groups", "outer"), None),
        check_vma=False,
    )
```

```python
import functools

import jax
import jax.numpy as jnp
from jax import lax
from jax.experimental import pallas as pl
from jax.experimental.pallas import tpu as pltpu
from jax.sharding import PartitionSpec as P

HEADS = 16
BLK = 128
WIN = 4
CHUNKS = 2


def passed_along(block, axis, distance):
    devices = range(lax.axis_size(axis))
    route = [(i - distance, i) for i in devices if i - distance in devices]
    return lax.ppermute(block, axis, route)


def from_partner(value, axis, stride):
    mask = 2**stride
    pairs = [(source, source ^ mask) for source in range(lax.axis_size(axis))]
    return lax.ppermute(value, axis, pairs)


def pick_blocks(source, block_index):
    return lax.dynamic_slice_in_dim(source, block_index[0] * BLK, BLK, 0)


def _nt(a, b):
    return lax.dot_general(a, b, (((1,), (1,)), ((), ())), preferred_element_type=jnp.float32)


def _nn(a, b):
    return lax.dot_general(a, b, (((1,), (0,)), ((), ())), preferred_element_type=jnp.float32)


def attend_kernel(level_count, meta, q_ref, ok_ref, ov_ref, pk_ref, pv_ref, *rest):
    far_refs = rest[: 2 * level_count]
    out_ref, bias_ref = rest[-2:]
    rows, head_dim = q_ref.shape
    panel_len = rows // BLK
    scale = head_dim ** (-0.5)

    @pl.when(pl.program_id(0) == 0)
    def _():
        row = lax.broadcasted_iota(jnp.int32, (rows, rows), 0)
        col = lax.broadcasted_iota(jnp.int32, (rows, rows), 1)
        q_blk = row // BLK
        k_blk = col // BLK
        width = jnp.zeros((rows, rows), jnp.int32)
        for r in range(panel_len):
            width = jnp.where(q_blk == r, meta[r], width)
        first_block = meta[panel_len]
        own_off = q_blk - k_blk
        own_vis = (own_off >= 0) & (own_off < width) & ((own_off > 0) | (col <= row))
        prev_off = q_blk + panel_len - k_blk
        prev_vis = (prev_off < width) & (first_block + q_blk - prev_off >= 0)
        bias_ref[:, :rows] = jnp.where(prev_vis, 0.0, -jnp.inf)
        bias_ref[:, rows:] = jnp.where(own_vis, 0.0, -jnp.inf)

    q = q_ref[...]
    s_prev = _nt(q, pk_ref[...]) * scale + bias_ref[:, :rows]
    s_own = _nt(q, ok_ref[...]) * scale + bias_ref[:, rows:]
    m_w = jnp.maximum(s_own.max(-1, keepdims=True), s_prev.max(-1, keepdims=True))
    e_own = jnp.exp(s_own - m_w)
    e_prev = jnp.exp(s_prev - m_w)
    l_w = e_own.sum(-1, keepdims=True) + e_prev.sum(-1, keepdims=True)
    o_w = _nn(e_own.astype(jnp.bfloat16), ov_ref[...]) + _nn(e_prev.astype(jnp.bfloat16), pv_ref[...])

    maxes, totals, sums = [m_w], [l_w], [o_w]
    for b in range(level_count):
        s = _nt(q, far_refs[2 * b][...]) * scale
        m = s.max(-1, keepdims=True)
        e = jnp.exp(s - m)
        maxes.append(m)
        totals.append(e.sum(-1, keepdims=True))
        sums.append(_nn(e.astype(jnp.bfloat16), far_refs[2 * b + 1][...]))

    top = maxes[0]
    for m in maxes[1:]:
        top = jnp.maximum(top, m)
    total = jnp.zeros_like(l_w)
    output = jnp.zeros_like(o_w)
    for m, l, o in zip(maxes, totals, sums):
        factor = jnp.exp(m - top)
        total = total + l * factor
        output = output + o * factor
    out_ref[...] = (output / total).astype(out_ref.dtype)


def attend(meta, queries, own_k, own_v, rim, far, first_head, prior=None):
    rows, features = queries.shape
    head_dim = features // HEADS
    heads = rim.shape[1] // head_dim
    level_count = len(far)
    far_rows = far[0].shape[0] // 2
    whole = pl.BlockSpec((rows, head_dim), lambda h, meta: (0, h + first_head))
    rim_k = pl.BlockSpec((rows, head_dim), lambda h, meta: (0, h))
    rim_v = pl.BlockSpec((rows, head_dim), lambda h, meta: (1, h))
    far_specs = []
    for _ in range(level_count):
        far_specs.append(pl.BlockSpec((far_rows, head_dim), lambda h, meta: (0, h)))
        far_specs.append(pl.BlockSpec((far_rows, head_dim), lambda h, meta: (1, h)))
    far_args = []
    for block in far:
        far_args += [block, block]
    keys = 2 * rows + level_count * far_rows
    args = [meta, queries, own_k, own_v, rim, rim, *far_args]
    in_specs = [whole] * 3 + [rim_k, rim_v] + far_specs
    aliases = {}
    if prior is not None:
        aliases = {len(args): 0}
        args.append(prior)
        in_specs.append(pl.BlockSpec(memory_space=pl.ANY))
    return pl.pallas_call(
        functools.partial(attend_kernel, level_count),
        out_shape=jax.ShapeDtypeStruct((rows, features), queries.dtype),
        grid_spec=pltpu.PrefetchScalarGridSpec(
            num_scalar_prefetch=1,
            grid=(heads,),
            in_specs=in_specs,
            out_specs=whole,
            scratch_shapes=[pltpu.VMEM((rows, 2 * rows), jnp.float32)],
        ),
        input_output_aliases=aliases,
        compiler_params=pltpu.CompilerParams(dimension_semantics=("arbitrary",)),
        cost_estimate=pl.CostEstimate(
            flops=4 * rows * keys * head_dim * heads,
            transcendentals=rows * keys * heads,
            bytes_accessed=2 * head_dim * heads * (6 * rows + 2 * level_count * far_rows),
        ),
    )(*args)


def on_device(queries, key_rows, value_rows, widths, columns):
    token_count, features = queries.shape
    panel_len = token_count // BLK
    device = lax.axis_index("outer")
    level_count = lax.axis_size("outer").bit_length() - 1
    meta = jnp.concatenate([widths, (device * panel_len)[None]]).astype(jnp.int32)
    wanted = [columns[jnp.bitwise_xor(device, 1 << b), b] - device * panel_len for b in range(level_count)]
    width = features // CHUNKS
    context = None
    for c in range(CHUNKS):
        cols = slice(c * width, (c + 1) * width)
        rim = passed_along(jnp.concatenate([key_rows[:, cols], value_rows[:, cols]], axis=0), "outer", 1)
        far = []
        for level_bit in range(level_count):
            outgoing = jnp.concatenate(
                [pick_blocks(key_rows, wanted[level_bit])[:, cols], pick_blocks(value_rows, wanted[level_bit])[:, cols]],
                axis=0,
            )
            far.append(from_partner(outgoing, "outer", level_bit))
        context = attend(
            meta, queries, key_rows, value_rows, rim, far, c * (HEADS // CHUNKS), context
        )
    return context


def solution(mesh):
    placed = (
        P(("groups", "outer"), None),
        P(("groups", "outer"), None),
        P(("groups", "outer"), None),
        P(("groups", "outer")),
        P("groups", None, None),
    )
    return jax.shard_map(
        on_device,
        mesh=mesh,
        in_specs=placed,
        out_specs=P(("groups", "outer"), None),
        check_vma=False,
    )
```

```python
import functools

import jax
import jax.numpy as jnp
from jax import lax
from jax.experimental import pallas as pl
from jax.experimental.pallas import tpu as pltpu
from jax.sharding import PartitionSpec as P

HEADS = 16
BLK = 128
WIN = 4
CHUNKS = 2


def passed_along(block, axis, distance):
    devices = range(lax.axis_size(axis))
    route = [(i - distance, i) for i in devices if i - distance in devices]
    return lax.ppermute(block, axis, route)


def from_partner(value, axis, stride):
    mask = 2**stride
    pairs = [(source, source ^ mask) for source in range(lax.axis_size(axis))]
    return lax.ppermute(value, axis, pairs)


def pick_blocks(source, block_index):
    return lax.dynamic_slice_in_dim(source, block_index[0] * BLK, BLK, 0)


def _nt(a, b):
    return lax.dot_general(a, b, (((1,), (1,)), ((), ())), preferred_element_type=jnp.float32)


def _nn(a, b):
    return lax.dot_general(a, b, (((1,), (0,)), ((), ())), preferred_element_type=jnp.float32)


def attend_kernel(level_count, meta, q_ref, ok_ref, ov_ref, pk_ref, pv_ref, tk_ref, tv_ref, *rest):
    far_refs = rest[: 2 * level_count]
    out_ref, bias_ref = rest[-2:]
    rows, head_dim = q_ref.shape
    panel_len = rows // BLK
    scale = head_dim ** (-0.5)

    @pl.when(pl.program_id(0) == 0)
    def _():
        row = lax.broadcasted_iota(jnp.int32, (rows, rows), 0)
        col = lax.broadcasted_iota(jnp.int32, (rows, rows), 1)
        q_blk = row // BLK
        k_blk = col // BLK
        width = jnp.zeros((rows, rows), jnp.int32)
        for r in range(panel_len):
            width = jnp.where(q_blk == r, meta[r], width)
        first_block = meta[panel_len]
        own_off = q_blk - k_blk
        own_vis = (own_off >= 0) & (own_off < width) & ((own_off > 0) | (col <= row))
        prev_blk = jnp.zeros((rows, rows), jnp.int32)
        for slot in range(panel_len):
            prev_blk = jnp.where(k_blk == slot, meta[panel_len + 1 + slot], prev_blk)
        prev_off = q_blk + panel_len - prev_blk
        prev_vis = (prev_off < width) & (first_block + q_blk - prev_off >= 0)
        bias_ref[:, :rows] = jnp.where(prev_vis, 0.0, -jnp.inf)
        bias_ref[:, rows:] = jnp.where(own_vis, 0.0, -jnp.inf)

    q = q_ref[...]
    pair = pk_ref.shape[0]
    s_prev = _nt(q, pk_ref[...]) * scale + bias_ref[:, :pair]
    s_third = _nt(q, tk_ref[...]) * scale + bias_ref[:, pair:rows]
    s_own = _nt(q, ok_ref[...]) * scale + bias_ref[:, rows:]
    m_w = jnp.maximum(
        jnp.maximum(s_own.max(-1, keepdims=True), s_prev.max(-1, keepdims=True)), s_third.max(-1, keepdims=True)
    )
    e_own = jnp.exp(s_own - m_w)
    e_prev = jnp.exp(s_prev - m_w)
    e_third = jnp.exp(s_third - m_w)
    l_w = e_own.sum(-1, keepdims=True) + e_prev.sum(-1, keepdims=True) + e_third.sum(-1, keepdims=True)
    o_w = (
        _nn(e_own.astype(jnp.bfloat16), ov_ref[...])
        + _nn(e_prev.astype(jnp.bfloat16), pv_ref[...])
        + _nn(e_third.astype(jnp.bfloat16), tv_ref[...])
    )

    maxes, totals, sums = [m_w], [l_w], [o_w]
    for b in range(level_count):
        s = _nt(q, far_refs[2 * b][...]) * scale
        m = s.max(-1, keepdims=True)
        e = jnp.exp(s - m)
        maxes.append(m)
        totals.append(e.sum(-1, keepdims=True))
        sums.append(_nn(e.astype(jnp.bfloat16), far_refs[2 * b + 1][...]))

    top = maxes[0]
    for m in maxes[1:]:
        top = jnp.maximum(top, m)
    total = jnp.zeros_like(l_w)
    output = jnp.zeros_like(o_w)
    for m, l, o in zip(maxes, totals, sums):
        factor = jnp.exp(m - top)
        total = total + l * factor
        output = output + o * factor
    out_ref[...] = (output / total).astype(out_ref.dtype)


def attend(meta, queries, own_k, own_v, pair, third, far, first_head, prior=None):
    rows, features = queries.shape
    head_dim = features // HEADS
    heads = pair.shape[1] // head_dim
    level_count = len(far)
    far_rows = far[0].shape[0] // 2
    whole = pl.BlockSpec((rows, head_dim), lambda h, meta: (0, h + first_head))
    pair_rows = pair.shape[0] // 2
    third_rows = third.shape[0] // 2
    pair_k = pl.BlockSpec((pair_rows, head_dim), lambda h, meta: (0, h))
    pair_v = pl.BlockSpec((pair_rows, head_dim), lambda h, meta: (1, h))
    third_k = pl.BlockSpec((third_rows, head_dim), lambda h, meta: (0, h))
    third_v = pl.BlockSpec((third_rows, head_dim), lambda h, meta: (1, h))
    far_specs = []
    for _ in range(level_count):
        far_specs.append(pl.BlockSpec((far_rows, head_dim), lambda h, meta: (0, h)))
        far_specs.append(pl.BlockSpec((far_rows, head_dim), lambda h, meta: (1, h)))
    far_args = []
    for block in far:
        far_args += [block, block]
    keys = 2 * rows + level_count * far_rows
    args = [meta, queries, own_k, own_v, pair, pair, third, third, *far_args]
    in_specs = [whole] * 3 + [pair_k, pair_v, third_k, third_v] + far_specs
    aliases = {}
    if prior is not None:
        aliases = {len(args): 0}
        args.append(prior)
        in_specs.append(pl.BlockSpec(memory_space=pl.ANY))
    return pl.pallas_call(
        functools.partial(attend_kernel, level_count),
        out_shape=jax.ShapeDtypeStruct((rows, features), queries.dtype),
        grid_spec=pltpu.PrefetchScalarGridSpec(
            num_scalar_prefetch=1,
            grid=(heads,),
            in_specs=in_specs,
            out_specs=whole,
            scratch_shapes=[pltpu.VMEM((rows, 2 * rows), jnp.float32)],
        ),
        input_output_aliases=aliases,
        compiler_params=pltpu.CompilerParams(dimension_semantics=("arbitrary",)),
        cost_estimate=pl.CostEstimate(
            flops=4 * rows * keys * head_dim * heads,
            transcendentals=rows * keys * heads,
            bytes_accessed=2 * head_dim * heads * (6 * rows + 2 * level_count * far_rows),
        ),
    )(*args)


def on_device(queries, key_rows, value_rows, widths, columns):
    token_count, features = queries.shape
    panel_len = token_count // BLK
    device = lax.axis_index("outer")
    level_count = lax.axis_size("outer").bit_length() - 1
    count = lax.axis_size("outer")
    wanted = [columns[jnp.bitwise_xor(device, 1 << b), b] - device * panel_len for b in range(level_count)]

    def relayed_block(sender):
        return jnp.where(sender % 2 == 1, wanted_of(sender), 0)

    def wanted_of(sender):
        return columns[jnp.bitwise_xor(sender, 1), 0, 0] - sender * panel_len

    def other_two(j):
        return jnp.where(j == 0, 1, 0), jnp.where(j == 2, 1, 2)

    mine_j = relayed_block(device)
    mine_a, mine_b = other_two(mine_j)
    sender = jnp.maximum(device - 1, 0)
    from_j = relayed_block(sender)
    from_a, from_b = other_two(from_j)
    meta = jnp.concatenate(
        [widths, jnp.stack([device * panel_len, from_a, from_b, from_j])]
    ).astype(jnp.int32)
    odd = device % 2 == 1
    even_pairs = [(i, i + 1) for i in range(0, count, 2) if i + 1 < count]
    forward_pairs = [(i, i + 2) for i in range(0, count, 2) if i + 2 < count]

    width = features // CHUNKS
    context = None
    for c in range(CHUNKS):
        cols = slice(c * width, (c + 1) * width)
        keys_c, values_c = key_rows[:, cols], value_rows[:, cols]
        far = []
        for level_bit in range(level_count):
            outgoing = jnp.concatenate(
                [pick_blocks(keys_c, wanted[level_bit]), pick_blocks(values_c, wanted[level_bit])], axis=0
            )
            far.append(from_partner(outgoing, "outer", level_bit))
        pair = passed_along(
            jnp.concatenate(
                [
                    pick_blocks(keys_c, mine_a[None]),
                    pick_blocks(keys_c, mine_b[None]),
                    pick_blocks(values_c, mine_a[None]),
                    pick_blocks(values_c, mine_b[None]),
                ],
                axis=0,
            ),
            "outer",
            1,
        )
        own_third = jnp.concatenate([keys_c[:BLK], values_c[:BLK]], axis=0)
        third_near = lax.ppermute(own_third, "outer", even_pairs)
        third_far = lax.ppermute(far[0], "outer", forward_pairs)
        third = jnp.where(odd, third_near, third_far)
        context = attend(meta, queries, key_rows, value_rows, pair, third, far, c * (HEADS // CHUNKS), context)
    return context


def solution(mesh):
    placed = (
        P(("groups", "outer"), None),
        P(("groups", "outer"), None),
        P(("groups", "outer"), None),
        P(("groups", "outer")),
        P("groups", None, None),
    )
    return jax.shard_map(
        on_device,
        mesh=mesh,
        in_specs=placed,
        out_specs=P(("groups", "outer"), None),
        check_vma=False,
    )
```

```python
import functools

import jax
import jax.numpy as jnp
from jax import lax
from jax.experimental import pallas as pl
from jax.experimental.pallas import tpu as pltpu
from jax.sharding import PartitionSpec as P

HEADS = 16
BLK = 128
WIN = 4
CHUNK_HEADS = (12, 4)


def passed_along(block, axis, distance):
    devices = range(lax.axis_size(axis))
    route = [(i - distance, i) for i in devices if i - distance in devices]
    return lax.ppermute(block, axis, route)


def from_partner(value, axis, stride):
    mask = 2**stride
    pairs = [(source, source ^ mask) for source in range(lax.axis_size(axis))]
    return lax.ppermute(value, axis, pairs)


def pick_blocks(source, block_index):
    return lax.dynamic_slice_in_dim(source, block_index[0] * BLK, BLK, 0)


def _nt(a, b):
    return lax.dot_general(a, b, (((1,), (1,)), ((), ())), preferred_element_type=jnp.float32)


def _nn(a, b):
    return lax.dot_general(a, b, (((1,), (0,)), ((), ())), preferred_element_type=jnp.float32)


def attend_kernel(level_count, meta, q_ref, ok_ref, ov_ref, pk_ref, pv_ref, *rest):
    far_refs = rest[: 2 * level_count]
    out_ref, bias_ref = rest[-2:]
    rows, head_dim = q_ref.shape
    panel_len = rows // BLK
    scale = head_dim ** (-0.5)

    @pl.when(pl.program_id(0) == 0)
    def _():
        row = lax.broadcasted_iota(jnp.int32, (rows, rows), 0)
        col = lax.broadcasted_iota(jnp.int32, (rows, rows), 1)
        q_blk = row // BLK
        k_blk = col // BLK
        width = jnp.zeros((rows, rows), jnp.int32)
        for r in range(panel_len):
            width = jnp.where(q_blk == r, meta[r], width)
        first_block = meta[panel_len]
        own_off = q_blk - k_blk
        own_vis = (own_off >= 0) & (own_off < width) & ((own_off > 0) | (col <= row))
        prev_off = q_blk + panel_len - k_blk
        prev_vis = (prev_off < width) & (first_block + q_blk - prev_off >= 0)
        bias_ref[:, :rows] = jnp.where(prev_vis, 0.0, -jnp.inf)
        bias_ref[:, rows:] = jnp.where(own_vis, 0.0, -jnp.inf)

    q = q_ref[...]
    s_prev = _nt(q, pk_ref[...]) * scale + bias_ref[:, :rows]
    s_own = _nt(q, ok_ref[...]) * scale + bias_ref[:, rows:]
    m_w = jnp.maximum(s_own.max(-1, keepdims=True), s_prev.max(-1, keepdims=True))
    e_own = jnp.exp(s_own - m_w)
    e_prev = jnp.exp(s_prev - m_w)
    l_w = e_own.sum(-1, keepdims=True) + e_prev.sum(-1, keepdims=True)
    o_w = _nn(e_own.astype(jnp.bfloat16), ov_ref[...]) + _nn(e_prev.astype(jnp.bfloat16), pv_ref[...])

    maxes, totals, sums = [m_w], [l_w], [o_w]
    for b in range(level_count):
        s = _nt(q, far_refs[2 * b][...]) * scale
        m = s.max(-1, keepdims=True)
        e = jnp.exp(s - m)
        maxes.append(m)
        totals.append(e.sum(-1, keepdims=True))
        sums.append(_nn(e.astype(jnp.bfloat16), far_refs[2 * b + 1][...]))

    top = maxes[0]
    for m in maxes[1:]:
        top = jnp.maximum(top, m)
    total = jnp.zeros_like(l_w)
    output = jnp.zeros_like(o_w)
    for m, l, o in zip(maxes, totals, sums):
        factor = jnp.exp(m - top)
        total = total + l * factor
        output = output + o * factor
    out_ref[...] = (output / total).astype(out_ref.dtype)


def attend(meta, queries, own_k, own_v, prev_k, prev_v, far, first_head, prior=None):
    rows, features = queries.shape
    head_dim = features // HEADS
    heads = prev_k.shape[1] // head_dim
    level_count = len(far)
    far_rows = far[0].shape[0] // 2
    whole = pl.BlockSpec((rows, head_dim), lambda h, meta: (0, h + first_head))
    part = pl.BlockSpec((rows, head_dim), lambda h, meta: (0, h))
    far_specs = []
    for _ in range(level_count):
        far_specs.append(pl.BlockSpec((far_rows, head_dim), lambda h, meta: (0, h)))
        far_specs.append(pl.BlockSpec((far_rows, head_dim), lambda h, meta: (1, h)))
    far_args = []
    for block in far:
        far_args += [block, block]
    keys = 2 * rows + level_count * far_rows
    args = [meta, queries, own_k, own_v, prev_k, prev_v, *far_args]
    in_specs = [whole] * 3 + [part] * 2 + far_specs
    aliases = {}
    if prior is not None:
        aliases = {len(args): 0}
        args.append(prior)
        in_specs.append(pl.BlockSpec(memory_space=pl.ANY))
    return pl.pallas_call(
        functools.partial(attend_kernel, level_count),
        out_shape=jax.ShapeDtypeStruct((rows, features), queries.dtype),
        grid_spec=pltpu.PrefetchScalarGridSpec(
            num_scalar_prefetch=1,
            grid=(heads,),
            in_specs=in_specs,
            out_specs=whole,
            scratch_shapes=[pltpu.VMEM((rows, 2 * rows), jnp.float32)],
        ),
        input_output_aliases=aliases,
        compiler_params=pltpu.CompilerParams(dimension_semantics=("arbitrary",)),
        cost_estimate=pl.CostEstimate(
            flops=4 * rows * keys * head_dim * heads,
            transcendentals=rows * keys * heads,
            bytes_accessed=2 * head_dim * heads * (6 * rows + 2 * level_count * far_rows),
        ),
    )(*args)


def on_device(queries, key_rows, value_rows, widths, columns):
    token_count, features = queries.shape
    panel_len = token_count // BLK
    device = lax.axis_index("outer")
    level_count = lax.axis_size("outer").bit_length() - 1
    meta = jnp.concatenate([widths, (device * panel_len)[None]]).astype(jnp.int32)
    wanted = [columns[jnp.bitwise_xor(device, 1 << b), b] - device * panel_len for b in range(level_count)]
    head_dim = features // HEADS
    context = None
    first_head = 0
    for heads in CHUNK_HEADS:
        cols = slice(first_head * head_dim, (first_head + heads) * head_dim)
        prev_keys, prev_values = passed_along((key_rows[:, cols], value_rows[:, cols]), "outer", 1)
        far = []
        for level_bit in range(level_count):
            outgoing = jnp.concatenate(
                [pick_blocks(key_rows, wanted[level_bit])[:, cols], pick_blocks(value_rows, wanted[level_bit])[:, cols]],
                axis=0,
            )
            far.append(from_partner(outgoing, "outer", level_bit))
        context = attend(meta, queries, key_rows, value_rows, prev_keys, prev_values, far, first_head, context)
        first_head += heads
    return context


def solution(mesh):
    placed = (
        P(("groups", "outer"), None),
        P(("groups", "outer"), None),
        P(("groups", "outer"), None),
        P(("groups", "outer")),
        P("groups", None, None),
    )
    return jax.shard_map(
        on_device,
        mesh=mesh,
        in_specs=placed,
        out_specs=P(("groups", "outer"), None),
        check_vma=False,
    )
```

```python
import functools

import jax
import jax.numpy as jnp
from jax import lax
from jax.experimental import pallas as pl
from jax.experimental.pallas import tpu as pltpu
from jax.sharding import PartitionSpec as P

HEADS = 16
BLK = 128
WIN = 4
CHUNK_HEADS = (12, 4)


def passed_along(block, axis, distance):
    devices = range(lax.axis_size(axis))
    route = [(i - distance, i) for i in devices if i - distance in devices]
    return lax.ppermute(block, axis, route)


def from_partner(value, axis, stride):
    mask = 2**stride
    pairs = [(source, source ^ mask) for source in range(lax.axis_size(axis))]
    return lax.ppermute(value, axis, pairs)


def pick_blocks(source, block_index):
    return lax.dynamic_slice_in_dim(source, block_index[0] * BLK, BLK, 0)


def _nt(a, b):
    return lax.dot_general(a, b, (((1,), (1,)), ((), ())), preferred_element_type=jnp.float32)


def _nn(a, b):
    return lax.dot_general(a, b, (((1,), (0,)), ((), ())), preferred_element_type=jnp.float32)


def attend_kernel(level_count, meta, q_ref, ok_ref, ov_ref, pk_ref, pv_ref, *rest):
    far_refs = rest[: 2 * level_count]
    out_ref, bias_ref = rest[-2:]
    rows, head_dim = q_ref.shape
    panel_len = rows // BLK
    scale = head_dim ** (-0.5)

    @pl.when(pl.program_id(0) == 0)
    def _():
        row = lax.broadcasted_iota(jnp.int32, (rows, rows), 0)
        col = lax.broadcasted_iota(jnp.int32, (rows, rows), 1)
        q_blk = row // BLK
        k_blk = col // BLK
        width = jnp.zeros((rows, rows), jnp.int32)
        for r in range(panel_len):
            width = jnp.where(q_blk == r, meta[r], width)
        first_block = meta[panel_len]
        own_off = q_blk - k_blk
        own_vis = (own_off >= 0) & (own_off < width) & ((own_off > 0) | (col <= row))
        prev_off = q_blk + panel_len - k_blk
        prev_vis = (prev_off < width) & (first_block + q_blk - prev_off >= 0)
        bias_ref[:, :rows] = jnp.where(prev_vis, 0.0, -jnp.inf)
        bias_ref[:, rows:] = jnp.where(own_vis, 0.0, -jnp.inf)

    q = q_ref[...]
    s_prev = _nt(q, pk_ref[...]) * scale + bias_ref[:, :rows]
    s_own = _nt(q, ok_ref[...]) * scale + bias_ref[:, rows:]
    m_w = jnp.maximum(s_own.max(-1, keepdims=True), s_prev.max(-1, keepdims=True))
    e_own = jnp.exp(s_own - m_w)
    e_prev = jnp.exp(s_prev - m_w)
    l_w = e_own.sum(-1, keepdims=True) + e_prev.sum(-1, keepdims=True)
    o_w = _nn(e_own.astype(jnp.bfloat16), ov_ref[...]) + _nn(e_prev.astype(jnp.bfloat16), pv_ref[...])

    maxes, totals, sums = [m_w], [l_w], [o_w]
    for b in range(level_count):
        s = _nt(q, far_refs[2 * b][...]) * scale
        m = s.max(-1, keepdims=True)
        e = jnp.exp(s - m)
        maxes.append(m)
        totals.append(e.sum(-1, keepdims=True))
        sums.append(_nn(e.astype(jnp.bfloat16), far_refs[2 * b + 1][...]))

    top = maxes[0]
    for m in maxes[1:]:
        top = jnp.maximum(top, m)
    total = jnp.zeros_like(l_w)
    output = jnp.zeros_like(o_w)
    for m, l, o in zip(maxes, totals, sums):
        factor = jnp.exp(m - top)
        total = total + l * factor
        output = output + o * factor
    out_ref[...] = (output / total).astype(out_ref.dtype)


def attend(meta, queries, own_k, own_v, prev_k, prev_v, far, first_head, prior=None):
    rows, features = queries.shape
    head_dim = features // HEADS
    heads = prev_k.shape[1] // head_dim
    level_count = len(far)
    far_rows = far[0].shape[0] // 2
    whole = pl.BlockSpec((rows, head_dim), lambda h, meta: (0, h + first_head))
    part = pl.BlockSpec((rows, head_dim), lambda h, meta: (0, h))
    far_specs = []
    for _ in range(level_count):
        far_specs.append(pl.BlockSpec((far_rows, head_dim), lambda h, meta: (0, h)))
        far_specs.append(pl.BlockSpec((far_rows, head_dim), lambda h, meta: (1, h)))
    far_args = []
    for block in far:
        far_args += [block, block]
    keys = 2 * rows + level_count * far_rows
    args = [meta, queries, own_k, own_v, prev_k, prev_v, *far_args]
    in_specs = [whole] * 3 + [part] * 2 + far_specs
    aliases = {}
    if prior is not None:
        aliases = {len(args): 0}
        args.append(prior)
        in_specs.append(pl.BlockSpec(memory_space=pl.ANY))
    return pl.pallas_call(
        functools.partial(attend_kernel, level_count),
        out_shape=jax.ShapeDtypeStruct((rows, features), queries.dtype),
        grid_spec=pltpu.PrefetchScalarGridSpec(
            num_scalar_prefetch=1,
            grid=(heads,),
            in_specs=in_specs,
            out_specs=whole,
            scratch_shapes=[pltpu.VMEM((rows, 2 * rows), jnp.float32)],
        ),
        input_output_aliases=aliases,
        compiler_params=pltpu.CompilerParams(dimension_semantics=("arbitrary",)),
        cost_estimate=pl.CostEstimate(
            flops=4 * rows * keys * head_dim * heads,
            transcendentals=rows * keys * heads,
            bytes_accessed=2 * head_dim * heads * (6 * rows + 2 * level_count * far_rows),
        ),
    )(*args)


def on_device(queries, key_rows, value_rows, widths, columns):
    token_count, features = queries.shape
    panel_len = token_count // BLK
    device = lax.axis_index("outer")
    level_count = lax.axis_size("outer").bit_length() - 1
    meta = jnp.concatenate([widths, (device * panel_len)[None]]).astype(jnp.int32)
    wanted = [columns[jnp.bitwise_xor(device, 1 << b), b] - device * panel_len for b in range(level_count)]
    head_dim = features // HEADS
    context = None
    first_head = 0
    arrived = ()
    for heads in CHUNK_HEADS:
        cols = slice(first_head * head_dim, (first_head + heads) * head_dim)
        key_src, value_src, *_ = lax.optimization_barrier((key_rows, value_rows, *arrived))
        prev_keys, prev_values = passed_along((key_src[:, cols], value_src[:, cols]), "outer", 1)
        far = []
        for level_bit in range(level_count):
            outgoing = jnp.concatenate(
                [pick_blocks(key_src, wanted[level_bit])[:, cols], pick_blocks(value_src, wanted[level_bit])[:, cols]],
                axis=0,
            )
            far.append(from_partner(outgoing, "outer", level_bit))
        context = attend(meta, queries, key_rows, value_rows, prev_keys, prev_values, far, first_head, context)
        arrived = (prev_keys, prev_values, *far)
        first_head += heads
    return context


def solution(mesh):
    placed = (
        P(("groups", "outer"), None),
        P(("groups", "outer"), None),
        P(("groups", "outer"), None),
        P(("groups", "outer")),
        P("groups", None, None),
    )
    return jax.shard_map(
        on_device,
        mesh=mesh,
        in_specs=placed,
        out_specs=P(("groups", "outer"), None),
        check_vma=False,
    )
```

```python
import functools

import jax
import jax.numpy as jnp
from jax import lax
from jax.experimental import pallas as pl
from jax.experimental.pallas import tpu as pltpu
from jax.sharding import PartitionSpec as P

HEADS = 16
BLK = 128
WIN = 4
LOG2E = 1.4426950408889634
CHUNKS = 2


def passed_along(block, axis, distance):
    devices = range(lax.axis_size(axis))
    route = [(i - distance, i) for i in devices if i - distance in devices]
    return lax.ppermute(block, axis, route)


def from_partner(value, axis, stride):
    mask = 2**stride
    pairs = [(source, source ^ mask) for source in range(lax.axis_size(axis))]
    return lax.ppermute(value, axis, pairs)


def pick_blocks(source, block_index):
    return lax.dynamic_slice_in_dim(source, block_index[0] * BLK, BLK, 0)


def _nt(a, b):
    return lax.dot_general(a, b, (((1,), (1,)), ((), ())), preferred_element_type=jnp.float32)


def _nn(a, b):
    return lax.dot_general(a, b, (((1,), (0,)), ((), ())), preferred_element_type=jnp.float32)


def attend_kernel(level_count, bias_ref, q_ref, ok_ref, ov_ref, pk_ref, pv_ref, *rest):
    far_refs = rest[: 2 * level_count]
    out_ref = rest[-1]
    rows, head_dim = q_ref.shape
    scale = head_dim ** (-0.5) * LOG2E

    q = q_ref[...]
    s_prev = _nt(q, pk_ref[...]) * scale + bias_ref[:, :rows]
    s_own = _nt(q, ok_ref[...]) * scale + bias_ref[:, rows:]
    m_w = jnp.maximum(s_own.max(-1, keepdims=True), s_prev.max(-1, keepdims=True))
    e_own = jnp.exp2(s_own - m_w)
    e_prev = jnp.exp2(s_prev - m_w)
    l_w = e_own.sum(-1, keepdims=True) + e_prev.sum(-1, keepdims=True)
    o_w = _nn(e_own.astype(jnp.bfloat16), ov_ref[...]) + _nn(e_prev.astype(jnp.bfloat16), pv_ref[...])

    maxes, totals, sums = [m_w], [l_w], [o_w]
    for b in range(level_count):
        s = _nt(q, far_refs[2 * b][...]) * scale
        m = s.max(-1, keepdims=True)
        e = jnp.exp2(s - m)
        maxes.append(m)
        totals.append(e.sum(-1, keepdims=True))
        sums.append(_nn(e.astype(jnp.bfloat16), far_refs[2 * b + 1][...]))

    top = maxes[0]
    for m in maxes[1:]:
        top = jnp.maximum(top, m)
    total = jnp.zeros_like(l_w)
    output = jnp.zeros_like(o_w)
    for m, l, o in zip(maxes, totals, sums):
        factor = jnp.exp2(m - top)
        total = total + l * factor
        output = output + o * factor
    out_ref[...] = (output / total).astype(out_ref.dtype)


def window_bias(widths, first_block, rows):
    panel_len = rows // BLK
    row = lax.broadcasted_iota(jnp.int32, (rows, rows), 0)
    col = lax.broadcasted_iota(jnp.int32, (rows, rows), 1)
    q_blk = row // BLK
    k_blk = col // BLK
    width = jnp.zeros((rows, rows), jnp.int32)
    for r in range(panel_len):
        width = jnp.where(q_blk == r, widths[r], width)
    own_off = q_blk - k_blk
    own_vis = (own_off >= 0) & (own_off < width) & ((own_off > 0) | (col <= row))
    prev_off = q_blk + panel_len - k_blk
    prev_vis = (prev_off < width) & (first_block + q_blk - prev_off >= 0)
    return jnp.concatenate(
        [jnp.where(prev_vis, 0.0, -jnp.inf), jnp.where(own_vis, 0.0, -jnp.inf)], axis=1
    ).astype(jnp.float32)


def attend(bias, queries, own_k, own_v, prev_k, prev_v, far, first_head, prior=None):
    rows, features = queries.shape
    head_dim = features // HEADS
    heads = prev_k.shape[1] // head_dim
    level_count = len(far)
    far_rows = far[0].shape[0] // 2
    whole = pl.BlockSpec((rows, head_dim), lambda h: (0, h + first_head))
    part = pl.BlockSpec((rows, head_dim), lambda h: (0, h))
    far_specs = []
    for _ in range(level_count):
        far_specs.append(pl.BlockSpec((far_rows, head_dim), lambda h: (0, h)))
        far_specs.append(pl.BlockSpec((far_rows, head_dim), lambda h: (1, h)))
    far_args = []
    for block in far:
        far_args += [block, block]
    keys = 2 * rows + level_count * far_rows
    args = [bias, queries, own_k, own_v, prev_k, prev_v, *far_args]
    in_specs = [pl.BlockSpec((rows, 2 * rows), lambda h: (0, 0))] + [whole] * 3 + [part] * 2 + far_specs
    aliases = {}
    if prior is not None:
        aliases = {len(args): 0}
        args.append(prior)
        in_specs.append(pl.BlockSpec(memory_space=pl.ANY))
    return pl.pallas_call(
        functools.partial(attend_kernel, level_count),
        out_shape=jax.ShapeDtypeStruct((rows, features), queries.dtype),
        grid=(heads,),
        in_specs=in_specs,
        out_specs=whole,
        input_output_aliases=aliases,
        compiler_params=pltpu.CompilerParams(dimension_semantics=("arbitrary",)),
        cost_estimate=pl.CostEstimate(
            flops=4 * rows * keys * head_dim * heads,
            transcendentals=rows * keys * heads,
            bytes_accessed=2 * head_dim * heads * (6 * rows + 2 * level_count * far_rows),
        ),
    )(*args)


def on_device(queries, key_rows, value_rows, widths, columns):
    token_count, features = queries.shape
    panel_len = token_count // BLK
    device = lax.axis_index("outer")
    level_count = lax.axis_size("outer").bit_length() - 1
    bias = window_bias(widths, device * panel_len, token_count)
    wanted = [columns[jnp.bitwise_xor(device, 1 << b), b] - device * panel_len for b in range(level_count)]
    width = features // CHUNKS
    context = None
    for c in range(CHUNKS):
        cols = slice(c * width, (c + 1) * width)
        prev_keys, prev_values = passed_along((key_rows[:, cols], value_rows[:, cols]), "outer", 1)
        far = []
        for level_bit in range(level_count):
            outgoing = jnp.concatenate(
                [pick_blocks(key_rows, wanted[level_bit])[:, cols], pick_blocks(value_rows, wanted[level_bit])[:, cols]],
                axis=0,
            )
            far.append(from_partner(outgoing, "outer", level_bit))
        context = attend(
            bias, queries, key_rows, value_rows, prev_keys, prev_values, far, c * (HEADS // CHUNKS), context
        )
    return context


def solution(mesh):
    placed = (
        P(("groups", "outer"), None),
        P(("groups", "outer"), None),
        P(("groups", "outer"), None),
        P(("groups", "outer")),
        P("groups", None, None),
    )
    return jax.shard_map(
        on_device,
        mesh=mesh,
        in_specs=placed,
        out_specs=P(("groups", "outer"), None),
        check_vma=False,
    )
```

```python
import functools

import jax
import jax.numpy as jnp
from jax import lax
from jax.experimental import pallas as pl
from jax.experimental.pallas import tpu as pltpu
from jax.sharding import PartitionSpec as P

HEADS = 16
BLK = 128
WIN = 4
CHUNKS = 2


def passed_along(block, axis, distance):
    devices = range(lax.axis_size(axis))
    route = [(i - distance, i) for i in devices if i - distance in devices]
    return lax.ppermute(block, axis, route)


def from_partner(value, axis, stride):
    mask = 2**stride
    pairs = [(source, source ^ mask) for source in range(lax.axis_size(axis))]
    return lax.ppermute(value, axis, pairs)


def pick_blocks(source, block_index):
    return lax.dynamic_slice_in_dim(source, block_index[0] * BLK, BLK, 0)


def _nt(a, b):
    return lax.dot_general(a, b, (((1,), (1,)), ((), ())), preferred_element_type=jnp.float32)


def _nn(a, b):
    return lax.dot_general(a, b, (((1,), (0,)), ((), ())), preferred_element_type=jnp.float32)


def attend_kernel(level_count, carry_in, carry_out, meta, q_ref, *rest):
    rows, head_dim = q_ref.shape
    panel_len = rows // BLK
    scale = head_dim ** (-0.5)
    q = q_ref[...]
    maxes, totals, sums = [], [], []
    rest = list(rest)
    if carry_in:
        sum_ref, stat_ref = rest[:2]
        rest = rest[2:]
        maxes.append(stat_ref[:, :1])
        totals.append(stat_ref[:, head_dim // 2 : head_dim // 2 + 1])
        sums.append(sum_ref[...])
    else:
        ok_ref, ov_ref, pk_ref, pv_ref = rest[:4]
        rest = rest[4:]
    far_refs = rest[: 2 * level_count]
    outs = rest[2 * level_count :]

    if not carry_in:
        bias_ref = outs[-1]
        outs = outs[:-1]

        @pl.when(pl.program_id(0) == 0)
        def _():
            row = lax.broadcasted_iota(jnp.int32, (rows, rows), 0)
            col = lax.broadcasted_iota(jnp.int32, (rows, rows), 1)
            q_blk = row // BLK
            k_blk = col // BLK
            width = jnp.zeros((rows, rows), jnp.int32)
            for r in range(panel_len):
                width = jnp.where(q_blk == r, meta[r], width)
            first_block = meta[panel_len]
            own_off = q_blk - k_blk
            own_vis = (own_off >= 0) & (own_off < width) & ((own_off > 0) | (col <= row))
            prev_off = q_blk + panel_len - k_blk
            prev_vis = (prev_off < width) & (first_block + q_blk - prev_off >= 0)
            bias_ref[:, :rows] = jnp.where(prev_vis, 0.0, -jnp.inf)
            bias_ref[:, rows:] = jnp.where(own_vis, 0.0, -jnp.inf)

        s_prev = _nt(q, pk_ref[...]) * scale + bias_ref[:, :rows]
        s_own = _nt(q, ok_ref[...]) * scale + bias_ref[:, rows:]
        m_w = jnp.maximum(s_own.max(-1, keepdims=True), s_prev.max(-1, keepdims=True))
        e_own = jnp.exp(s_own - m_w)
        e_prev = jnp.exp(s_prev - m_w)
        maxes.append(m_w)
        totals.append(e_own.sum(-1, keepdims=True) + e_prev.sum(-1, keepdims=True))
        sums.append(_nn(e_own.astype(jnp.bfloat16), ov_ref[...]) + _nn(e_prev.astype(jnp.bfloat16), pv_ref[...]))

    for b in range(level_count):
        s = _nt(q, far_refs[2 * b][...]) * scale
        m = s.max(-1, keepdims=True)
        e = jnp.exp(s - m)
        maxes.append(m)
        totals.append(e.sum(-1, keepdims=True))
        sums.append(_nn(e.astype(jnp.bfloat16), far_refs[2 * b + 1][...]))

    top = maxes[0]
    for m in maxes[1:]:
        top = jnp.maximum(top, m)
    total = jnp.zeros_like(totals[0])
    output = jnp.zeros_like(sums[0])
    for m, l, o in zip(maxes, totals, sums):
        factor = jnp.exp(m - top)
        total = total + l * factor
        output = output + o * factor
    if carry_out:
        sum_out, stat_out = outs[-2:]
        sum_out[...] = output
        lane = lax.broadcasted_iota(jnp.int32, stat_out.shape, 1)
        stat_out[...] = jnp.where(lane < head_dim // 2, top, total)
    else:
        outs[-1][...] = (output / total).astype(outs[-1].dtype)


def attend(meta, queries, own, far, first_head, prior=None, carry=None, carry_out=False):
    rows, features = queries.shape
    head_dim = features // HEADS
    width = (carry[0] if carry is not None else own[2]).shape[1]
    heads = width // head_dim
    level_count = len(far)
    whole = pl.BlockSpec((rows, head_dim), lambda h, meta: (0, h + first_head))
    part = pl.BlockSpec((rows, head_dim), lambda h, meta: (0, h))
    args, in_specs = [meta, queries], [whole]
    if carry is not None:
        args += list(carry)
        in_specs += [part, part]
    else:
        args += list(own)
        in_specs += [whole, whole, part, part]
    for block in far:
        far_rows = block.shape[0] // 2
        args += [block, block]
        in_specs.append(pl.BlockSpec((far_rows, head_dim), lambda h, meta: (0, h)))
        in_specs.append(pl.BlockSpec((far_rows, head_dim), lambda h, meta: (1, h)))
    aliases = {}
    if carry_out:
        out_shape = (jax.ShapeDtypeStruct((rows, width), jnp.float32),) * 2
        out_specs = (part, part)
    else:
        out_shape = jax.ShapeDtypeStruct((rows, features), queries.dtype)
        out_specs = whole
        if prior is not None:
            aliases = {len(args): 0}
            args.append(prior)
            in_specs.append(pl.BlockSpec(memory_space=pl.ANY))
    scratch = [] if carry is not None else [pltpu.VMEM((rows, 2 * rows), jnp.float32)]
    keys = (0 if carry is not None else 2 * rows) + level_count * BLK
    return pl.pallas_call(
        functools.partial(attend_kernel, level_count, carry is not None, carry_out),
        out_shape=out_shape,
        grid_spec=pltpu.PrefetchScalarGridSpec(
            num_scalar_prefetch=1,
            grid=(heads,),
            in_specs=in_specs,
            out_specs=out_specs,
            scratch_shapes=scratch,
        ),
        input_output_aliases=aliases,
        compiler_params=pltpu.CompilerParams(dimension_semantics=("arbitrary",)),
        cost_estimate=pl.CostEstimate(
            flops=4 * rows * keys * head_dim * heads,
            transcendentals=rows * keys * heads,
            bytes_accessed=2 * head_dim * heads * (6 * rows + 2 * keys) + 16 * rows * width,
        ),
    )(*args)


def on_device(queries, key_rows, value_rows, widths, columns):
    token_count, features = queries.shape
    panel_len = token_count // BLK
    device = lax.axis_index("outer")
    level_count = lax.axis_size("outer").bit_length() - 1
    meta = jnp.concatenate([widths, (device * panel_len)[None]]).astype(jnp.int32)
    wanted = [columns[jnp.bitwise_xor(device, 1 << b), b] - device * panel_len for b in range(level_count)]
    width = features // CHUNKS
    context = None
    for c in range(CHUNKS):
        cols = slice(c * width, (c + 1) * width)
        prev_keys, prev_values = passed_along((key_rows[:, cols], value_rows[:, cols]), "outer", 1)
        far = []
        for level_bit in range(level_count):
            outgoing = jnp.concatenate(
                [pick_blocks(key_rows, wanted[level_bit])[:, cols], pick_blocks(value_rows, wanted[level_bit])[:, cols]],
                axis=0,
            )
            far.append(from_partner(outgoing, "outer", level_bit))
        own = (key_rows, value_rows, prev_keys, prev_values)
        first_head = c * (HEADS // CHUNKS)
        if c < CHUNKS - 1:
            context = attend(meta, queries, own, far, first_head, context)
        else:
            carry = attend(meta, queries, own, far[:-1], first_head, carry_out=True)
            context = attend(meta, queries, None, far[-1:], first_head, context, carry=carry)
    return context


def solution(mesh):
    placed = (
        P(("groups", "outer"), None),
        P(("groups", "outer"), None),
        P(("groups", "outer"), None),
        P(("groups", "outer")),
        P("groups", None, None),
    )
    return jax.shard_map(
        on_device,
        mesh=mesh,
        in_specs=placed,
        out_specs=P(("groups", "outer"), None),
        check_vma=False,
    )
```

```python
import functools

import jax
import jax.numpy as jnp
from jax import lax
from jax.experimental import pallas as pl
from jax.experimental.pallas import tpu as pltpu
from jax.sharding import PartitionSpec as P

HEADS = 16
BLK = 128
WIN = 4
HDIM = 128
HEADS_PER_STEP = 2
CHUNKS = 2


def passed_along(block, axis, distance):
    devices = range(lax.axis_size(axis))
    route = [(i - distance, i) for i in devices if i - distance in devices]
    return lax.ppermute(block, axis, route)


def from_partner(value, axis, stride):
    mask = 2**stride
    pairs = [(source, source ^ mask) for source in range(lax.axis_size(axis))]
    return lax.ppermute(value, axis, pairs)


def pick_blocks(source, block_index):
    return lax.dynamic_slice_in_dim(source, block_index[0] * BLK, BLK, 0)


def _nt(a, b):
    return lax.dot_general(a, b, (((1,), (1,)), ((), ())), preferred_element_type=jnp.float32)


def _nn(a, b):
    return lax.dot_general(a, b, (((1,), (0,)), ((), ())), preferred_element_type=jnp.float32)


def attend_kernel(level_count, meta, q_ref, ok_ref, ov_ref, pk_ref, pv_ref, *rest):
    far_refs = rest[: 2 * level_count]
    out_ref, bias_ref = rest[-2:]
    rows = q_ref.shape[0]
    head_dim = HDIM
    panel_len = rows // BLK
    scale = head_dim ** (-0.5)

    @pl.when(pl.program_id(0) == 0)
    def _():
        row = lax.broadcasted_iota(jnp.int32, (rows, rows), 0)
        col = lax.broadcasted_iota(jnp.int32, (rows, rows), 1)
        q_blk = row // BLK
        k_blk = col // BLK
        width = jnp.zeros((rows, rows), jnp.int32)
        for r in range(panel_len):
            width = jnp.where(q_blk == r, meta[r], width)
        first_block = meta[panel_len]
        own_off = q_blk - k_blk
        own_vis = (own_off >= 0) & (own_off < width) & ((own_off > 0) | (col <= row))
        prev_off = q_blk + panel_len - k_blk
        prev_vis = (prev_off < width) & (first_block + q_blk - prev_off >= 0)
        bias_ref[:, :rows] = jnp.where(prev_vis, 0.0, -jnp.inf)
        bias_ref[:, rows:] = jnp.where(own_vis, 0.0, -jnp.inf)

    for sub in range(q_ref.shape[1] // head_dim):
        cols = slice(sub * head_dim, (sub + 1) * head_dim)
        q = q_ref[:, cols]
        s_prev = _nt(q, pk_ref[:, cols]) * scale + bias_ref[:, :rows]
        s_own = _nt(q, ok_ref[:, cols]) * scale + bias_ref[:, rows:]
        m_w = jnp.maximum(s_own.max(-1, keepdims=True), s_prev.max(-1, keepdims=True))
        e_own = jnp.exp(s_own - m_w)
        e_prev = jnp.exp(s_prev - m_w)
        l_w = e_own.sum(-1, keepdims=True) + e_prev.sum(-1, keepdims=True)
        o_w = _nn(e_own.astype(jnp.bfloat16), ov_ref[:, cols]) + _nn(e_prev.astype(jnp.bfloat16), pv_ref[:, cols])

        maxes, totals, sums = [m_w], [l_w], [o_w]
        for b in range(level_count):
            s = _nt(q, far_refs[2 * b][:, cols]) * scale
            m = s.max(-1, keepdims=True)
            e = jnp.exp(s - m)
            maxes.append(m)
            totals.append(e.sum(-1, keepdims=True))
            sums.append(_nn(e.astype(jnp.bfloat16), far_refs[2 * b + 1][:, cols]))

        top = maxes[0]
        for m in maxes[1:]:
            top = jnp.maximum(top, m)
        total = jnp.zeros_like(l_w)
        output = jnp.zeros_like(o_w)
        for m, l, o in zip(maxes, totals, sums):
            factor = jnp.exp(m - top)
            total = total + l * factor
            output = output + o * factor
        out_ref[:, cols] = (output / total).astype(out_ref.dtype)


def attend(meta, queries, own_k, own_v, prev_k, prev_v, far, first_head, prior=None):
    rows, features = queries.shape
    head_dim = features // HEADS
    block = head_dim * HEADS_PER_STEP
    heads = prev_k.shape[1] // block
    first_head = first_head // HEADS_PER_STEP
    level_count = len(far)
    far_rows = far[0].shape[0] // 2
    whole = pl.BlockSpec((rows, block), lambda h, meta: (0, h + first_head))
    part = pl.BlockSpec((rows, block), lambda h, meta: (0, h))
    far_specs = []
    for _ in range(level_count):
        far_specs.append(pl.BlockSpec((far_rows, block), lambda h, meta: (0, h)))
        far_specs.append(pl.BlockSpec((far_rows, block), lambda h, meta: (1, h)))
    far_args = []
    for arrived in far:
        far_args += [arrived, arrived]
    keys = 2 * rows + level_count * far_rows
    args = [meta, queries, own_k, own_v, prev_k, prev_v, *far_args]
    in_specs = [whole] * 3 + [part] * 2 + far_specs
    aliases = {}
    if prior is not None:
        aliases = {len(args): 0}
        args.append(prior)
        in_specs.append(pl.BlockSpec(memory_space=pl.ANY))
    return pl.pallas_call(
        functools.partial(attend_kernel, level_count),
        out_shape=jax.ShapeDtypeStruct((rows, features), queries.dtype),
        grid_spec=pltpu.PrefetchScalarGridSpec(
            num_scalar_prefetch=1,
            grid=(heads,),
            in_specs=in_specs,
            out_specs=whole,
            scratch_shapes=[pltpu.VMEM((rows, 2 * rows), jnp.float32)],
        ),
        input_output_aliases=aliases,
        compiler_params=pltpu.CompilerParams(dimension_semantics=("arbitrary",)),
        cost_estimate=pl.CostEstimate(
            flops=4 * rows * keys * head_dim * HEADS_PER_STEP * heads,
            transcendentals=rows * keys * heads * HEADS_PER_STEP,
            bytes_accessed=2 * head_dim * HEADS_PER_STEP * heads * (6 * rows + 2 * level_count * far_rows),
        ),
    )(*args)


def on_device(queries, key_rows, value_rows, widths, columns):
    token_count, features = queries.shape
    panel_len = token_count // BLK
    device = lax.axis_index("outer")
    level_count = lax.axis_size("outer").bit_length() - 1
    meta = jnp.concatenate([widths, (device * panel_len)[None]]).astype(jnp.int32)
    wanted = [columns[jnp.bitwise_xor(device, 1 << b), b] - device * panel_len for b in range(level_count)]
    width = features // CHUNKS
    context = None
    for c in range(CHUNKS):
        cols = slice(c * width, (c + 1) * width)
        prev_keys, prev_values = passed_along((key_rows[:, cols], value_rows[:, cols]), "outer", 1)
        far = []
        for level_bit in range(level_count):
            outgoing = jnp.concatenate(
                [pick_blocks(key_rows, wanted[level_bit])[:, cols], pick_blocks(value_rows, wanted[level_bit])[:, cols]],
                axis=0,
            )
            far.append(from_partner(outgoing, "outer", level_bit))
        context = attend(
            meta, queries, key_rows, value_rows, prev_keys, prev_values, far, c * (HEADS // CHUNKS), context
        )
    return context


def solution(mesh):
    placed = (
        P(("groups", "outer"), None),
        P(("groups", "outer"), None),
        P(("groups", "outer"), None),
        P(("groups", "outer")),
        P("groups", None, None),
    )
    return jax.shard_map(
        on_device,
        mesh=mesh,
        in_specs=placed,
        out_specs=P(("groups", "outer"), None),
        check_vma=False,
    )
```

```python
import functools

import jax
import jax.numpy as jnp
from jax import lax
from jax.experimental import pallas as pl
from jax.experimental.pallas import tpu as pltpu
from jax.sharding import PartitionSpec as P

HEADS = 16
BLK = 128
WIN = 4
HDIM = 128
HEADS_PER_STEP = 4
CHUNKS = 2


def passed_along(block, axis, distance):
    devices = range(lax.axis_size(axis))
    route = [(i - distance, i) for i in devices if i - distance in devices]
    return lax.ppermute(block, axis, route)


def from_partner(value, axis, stride):
    mask = 2**stride
    pairs = [(source, source ^ mask) for source in range(lax.axis_size(axis))]
    return lax.ppermute(value, axis, pairs)


def pick_blocks(source, block_index):
    return lax.dynamic_slice_in_dim(source, block_index[0] * BLK, BLK, 0)


def _nt(a, b):
    return lax.dot_general(a, b, (((1,), (1,)), ((), ())), preferred_element_type=jnp.float32)


def _nn(a, b):
    return lax.dot_general(a, b, (((1,), (0,)), ((), ())), preferred_element_type=jnp.float32)


def attend_kernel(level_count, meta, q_ref, ok_ref, ov_ref, pk_ref, pv_ref, *rest):
    far_refs = rest[: 2 * level_count]
    out_ref, bias_ref = rest[-2:]
    rows = q_ref.shape[0]
    head_dim = HDIM
    panel_len = rows // BLK
    scale = head_dim ** (-0.5)

    @pl.when(pl.program_id(0) == 0)
    def _():
        row = lax.broadcasted_iota(jnp.int32, (rows, rows), 0)
        col = lax.broadcasted_iota(jnp.int32, (rows, rows), 1)
        q_blk = row // BLK
        k_blk = col // BLK
        width = jnp.zeros((rows, rows), jnp.int32)
        for r in range(panel_len):
            width = jnp.where(q_blk == r, meta[r], width)
        first_block = meta[panel_len]
        own_off = q_blk - k_blk
        own_vis = (own_off >= 0) & (own_off < width) & ((own_off > 0) | (col <= row))
        prev_off = q_blk + panel_len - k_blk
        prev_vis = (prev_off < width) & (first_block + q_blk - prev_off >= 0)
        bias_ref[:, :rows] = jnp.where(prev_vis, 0.0, -jnp.inf)
        bias_ref[:, rows:] = jnp.where(own_vis, 0.0, -jnp.inf)

    for sub in range(q_ref.shape[1] // head_dim):
        cols = slice(sub * head_dim, (sub + 1) * head_dim)
        q = q_ref[:, cols]
        s_prev = _nt(q, pk_ref[:, cols]) * scale + bias_ref[:, :rows]
        s_own = _nt(q, ok_ref[:, cols]) * scale + bias_ref[:, rows:]
        m_w = jnp.maximum(s_own.max(-1, keepdims=True), s_prev.max(-1, keepdims=True))
        e_own = jnp.exp(s_own - m_w)
        e_prev = jnp.exp(s_prev - m_w)
        l_w = e_own.sum(-1, keepdims=True) + e_prev.sum(-1, keepdims=True)
        o_w = _nn(e_own.astype(jnp.bfloat16), ov_ref[:, cols]) + _nn(e_prev.astype(jnp.bfloat16), pv_ref[:, cols])

        maxes, totals, sums = [m_w], [l_w], [o_w]
        for b in range(level_count):
            s = _nt(q, far_refs[2 * b][:, cols]) * scale
            m = s.max(-1, keepdims=True)
            e = jnp.exp(s - m)
            maxes.append(m)
            totals.append(e.sum(-1, keepdims=True))
            sums.append(_nn(e.astype(jnp.bfloat16), far_refs[2 * b + 1][:, cols]))

        top = maxes[0]
        for m in maxes[1:]:
            top = jnp.maximum(top, m)
        total = jnp.zeros_like(l_w)
        output = jnp.zeros_like(o_w)
        for m, l, o in zip(maxes, totals, sums):
            factor = jnp.exp(m - top)
            total = total + l * factor
            output = output + o * factor
        out_ref[:, cols] = (output / total).astype(out_ref.dtype)


def attend(meta, queries, own_k, own_v, prev_k, prev_v, far, first_head, prior=None):
    rows, features = queries.shape
    head_dim = features // HEADS
    block = head_dim * HEADS_PER_STEP
    heads = prev_k.shape[1] // block
    first_head = first_head // HEADS_PER_STEP
    level_count = len(far)
    far_rows = far[0].shape[0] // 2
    whole = pl.BlockSpec((rows, block), lambda h, meta: (0, h + first_head))
    part = pl.BlockSpec((rows, block), lambda h, meta: (0, h))
    far_specs = []
    for _ in range(level_count):
        far_specs.append(pl.BlockSpec((far_rows, block), lambda h, meta: (0, h)))
        far_specs.append(pl.BlockSpec((far_rows, block), lambda h, meta: (1, h)))
    far_args = []
    for arrived in far:
        far_args += [arrived, arrived]
    keys = 2 * rows + level_count * far_rows
    args = [meta, queries, own_k, own_v, prev_k, prev_v, *far_args]
    in_specs = [whole] * 3 + [part] * 2 + far_specs
    aliases = {}
    if prior is not None:
        aliases = {len(args): 0}
        args.append(prior)
        in_specs.append(pl.BlockSpec(memory_space=pl.ANY))
    return pl.pallas_call(
        functools.partial(attend_kernel, level_count),
        out_shape=jax.ShapeDtypeStruct((rows, features), queries.dtype),
        grid_spec=pltpu.PrefetchScalarGridSpec(
            num_scalar_prefetch=1,
            grid=(heads,),
            in_specs=in_specs,
            out_specs=whole,
            scratch_shapes=[pltpu.VMEM((rows, 2 * rows), jnp.float32)],
        ),
        input_output_aliases=aliases,
        compiler_params=pltpu.CompilerParams(dimension_semantics=("arbitrary",)),
        cost_estimate=pl.CostEstimate(
            flops=4 * rows * keys * head_dim * HEADS_PER_STEP * heads,
            transcendentals=rows * keys * heads * HEADS_PER_STEP,
            bytes_accessed=2 * head_dim * HEADS_PER_STEP * heads * (6 * rows + 2 * level_count * far_rows),
        ),
    )(*args)


def on_device(queries, key_rows, value_rows, widths, columns):
    token_count, features = queries.shape
    panel_len = token_count // BLK
    device = lax.axis_index("outer")
    level_count = lax.axis_size("outer").bit_length() - 1
    meta = jnp.concatenate([widths, (device * panel_len)[None]]).astype(jnp.int32)
    wanted = [columns[jnp.bitwise_xor(device, 1 << b), b] - device * panel_len for b in range(level_count)]
    width = features // CHUNKS
    context = None
    for c in range(CHUNKS):
        cols = slice(c * width, (c + 1) * width)
        prev_keys, prev_values = passed_along((key_rows[:, cols], value_rows[:, cols]), "outer", 1)
        far = []
        for level_bit in range(level_count):
            outgoing = jnp.concatenate(
                [pick_blocks(key_rows, wanted[level_bit])[:, cols], pick_blocks(value_rows, wanted[level_bit])[:, cols]],
                axis=0,
            )
            far.append(from_partner(outgoing, "outer", level_bit))
        context = attend(
            meta, queries, key_rows, value_rows, prev_keys, prev_values, far, c * (HEADS // CHUNKS), context
        )
    return context


def solution(mesh):
    placed = (
        P(("groups", "outer"), None),
        P(("groups", "outer"), None),
        P(("groups", "outer"), None),
        P(("groups", "outer")),
        P("groups", None, None),
    )
    return jax.shard_map(
        on_device,
        mesh=mesh,
        in_specs=placed,
        out_specs=P(("groups", "outer"), None),
        check_vma=False,
    )
```

```python
import functools

import jax
import jax.numpy as jnp
from jax import lax
from jax.experimental import pallas as pl
from jax.experimental.pallas import tpu as pltpu
from jax.sharding import PartitionSpec as P

HEADS = 16
BLK = 128
WIN = 4
HDIM = 128
LOG2E = 1.4426950408889634
HEADS_PER_STEP = 4
CHUNKS = 2


def passed_along(block, axis, distance):
    devices = range(lax.axis_size(axis))
    route = [(i - distance, i) for i in devices if i - distance in devices]
    return lax.ppermute(block, axis, route)


def from_partner(value, axis, stride):
    mask = 2**stride
    pairs = [(source, source ^ mask) for source in range(lax.axis_size(axis))]
    return lax.ppermute(value, axis, pairs)


def pick_blocks(source, block_index):
    return lax.dynamic_slice_in_dim(source, block_index[0] * BLK, BLK, 0)


def _nt(a, b):
    return lax.dot_general(a, b, (((1,), (1,)), ((), ())), preferred_element_type=jnp.float32)


def _nn(a, b):
    return lax.dot_general(a, b, (((1,), (0,)), ((), ())), preferred_element_type=jnp.float32)


def attend_kernel(level_count, meta, q_ref, ok_ref, ov_ref, pk_ref, pv_ref, *rest):
    far_refs = rest[: 2 * level_count]
    out_ref, bias_ref = rest[-2:]
    rows = q_ref.shape[0]
    head_dim = HDIM
    panel_len = rows // BLK
    scale = head_dim ** (-0.5) * LOG2E

    @pl.when(pl.program_id(0) == 0)
    def _():
        row = lax.broadcasted_iota(jnp.int32, (rows, rows), 0)
        col = lax.broadcasted_iota(jnp.int32, (rows, rows), 1)
        q_blk = row // BLK
        k_blk = col // BLK
        width = jnp.zeros((rows, rows), jnp.int32)
        for r in range(panel_len):
            width = jnp.where(q_blk == r, meta[r], width)
        first_block = meta[panel_len]
        own_off = q_blk - k_blk
        own_vis = (own_off >= 0) & (own_off < width) & ((own_off > 0) | (col <= row))
        prev_off = q_blk + panel_len - k_blk
        prev_vis = (prev_off < width) & (first_block + q_blk - prev_off >= 0)
        bias_ref[:, :rows] = jnp.where(prev_vis, 0.0, -jnp.inf)
        bias_ref[:, rows:] = jnp.where(own_vis, 0.0, -jnp.inf)

    for sub in range(q_ref.shape[1] // head_dim):
        cols = slice(sub * head_dim, (sub + 1) * head_dim)
        q = q_ref[:, cols]
        s_prev = _nt(q, pk_ref[:, cols]) * scale + bias_ref[:, :rows]
        s_own = _nt(q, ok_ref[:, cols]) * scale + bias_ref[:, rows:]
        m_w = jnp.maximum(s_own.max(-1, keepdims=True), s_prev.max(-1, keepdims=True))
        e_own = jnp.exp2(s_own - m_w)
        e_prev = jnp.exp2(s_prev - m_w)
        l_w = e_own.sum(-1, keepdims=True) + e_prev.sum(-1, keepdims=True)
        o_w = _nn(e_own.astype(jnp.bfloat16), ov_ref[:, cols]) + _nn(e_prev.astype(jnp.bfloat16), pv_ref[:, cols])

        maxes, totals, sums = [m_w], [l_w], [o_w]
        for b in range(level_count):
            s = _nt(q, far_refs[2 * b][:, cols]) * scale
            m = s.max(-1, keepdims=True)
            e = jnp.exp2(s - m)
            maxes.append(m)
            totals.append(e.sum(-1, keepdims=True))
            sums.append(_nn(e.astype(jnp.bfloat16), far_refs[2 * b + 1][:, cols]))

        top = maxes[0]
        for m in maxes[1:]:
            top = jnp.maximum(top, m)
        total = jnp.zeros_like(l_w)
        output = jnp.zeros_like(o_w)
        for m, l, o in zip(maxes, totals, sums):
            factor = jnp.exp2(m - top)
            total = total + l * factor
            output = output + o * factor
        out_ref[:, cols] = (output / total).astype(out_ref.dtype)


def attend(meta, queries, own_k, own_v, prev_k, prev_v, far, first_head, prior=None):
    rows, features = queries.shape
    head_dim = features // HEADS
    block = head_dim * HEADS_PER_STEP
    heads = prev_k.shape[1] // block
    first_head = first_head // HEADS_PER_STEP
    level_count = len(far)
    far_rows = far[0].shape[0] // 2
    whole = pl.BlockSpec((rows, block), lambda h, meta: (0, h + first_head))
    part = pl.BlockSpec((rows, block), lambda h, meta: (0, h))
    far_specs = []
    for _ in range(level_count):
        far_specs.append(pl.BlockSpec((far_rows, block), lambda h, meta: (0, h)))
        far_specs.append(pl.BlockSpec((far_rows, block), lambda h, meta: (1, h)))
    far_args = []
    for arrived in far:
        far_args += [arrived, arrived]
    keys = 2 * rows + level_count * far_rows
    args = [meta, queries, own_k, own_v, prev_k, prev_v, *far_args]
    in_specs = [whole] * 3 + [part] * 2 + far_specs
    aliases = {}
    if prior is not None:
        aliases = {len(args): 0}
        args.append(prior)
        in_specs.append(pl.BlockSpec(memory_space=pl.ANY))
    return pl.pallas_call(
        functools.partial(attend_kernel, level_count),
        out_shape=jax.ShapeDtypeStruct((rows, features), queries.dtype),
        grid_spec=pltpu.PrefetchScalarGridSpec(
            num_scalar_prefetch=1,
            grid=(heads,),
            in_specs=in_specs,
            out_specs=whole,
            scratch_shapes=[pltpu.VMEM((rows, 2 * rows), jnp.float32)],
        ),
        input_output_aliases=aliases,
        compiler_params=pltpu.CompilerParams(dimension_semantics=("arbitrary",)),
        cost_estimate=pl.CostEstimate(
            flops=4 * rows * keys * head_dim * HEADS_PER_STEP * heads,
            transcendentals=rows * keys * heads * HEADS_PER_STEP,
            bytes_accessed=2 * head_dim * HEADS_PER_STEP * heads * (6 * rows + 2 * level_count * far_rows),
        ),
    )(*args)


def on_device(queries, key_rows, value_rows, widths, columns):
    token_count, features = queries.shape
    panel_len = token_count // BLK
    device = lax.axis_index("outer")
    level_count = lax.axis_size("outer").bit_length() - 1
    meta = jnp.concatenate([widths, (device * panel_len)[None]]).astype(jnp.int32)
    wanted = [columns[jnp.bitwise_xor(device, 1 << b), b] - device * panel_len for b in range(level_count)]
    width = features // CHUNKS
    context = None
    for c in range(CHUNKS):
        cols = slice(c * width, (c + 1) * width)
        prev_keys, prev_values = passed_along((key_rows[:, cols], value_rows[:, cols]), "outer", 1)
        far = []
        for level_bit in range(level_count):
            outgoing = jnp.concatenate(
                [pick_blocks(key_rows, wanted[level_bit])[:, cols], pick_blocks(value_rows, wanted[level_bit])[:, cols]],
                axis=0,
            )
            far.append(from_partner(outgoing, "outer", level_bit))
        context = attend(
            meta, queries, key_rows, value_rows, prev_keys, prev_values, far, c * (HEADS // CHUNKS), context
        )
    return context


def solution(mesh):
    placed = (
        P(("groups", "outer"), None),
        P(("groups", "outer"), None),
        P(("groups", "outer"), None),
        P(("groups", "outer")),
        P("groups", None, None),
    )
    return jax.shard_map(
        on_device,
        mesh=mesh,
        in_specs=placed,
        out_specs=P(("groups", "outer"), None),
        check_vma=False,
    )
```

```python
import functools

import jax
import jax.numpy as jnp
from jax import lax
from jax.experimental import pallas as pl
from jax.experimental.pallas import tpu as pltpu
from jax.sharding import PartitionSpec as P

HEADS = 16
BLK = 128
WIN = 4
HDIM = 128
LOG2E = 1.4426950408889634
HEADS_PER_STEP = 4
CHUNKS = 2


def passed_along(block, axis, distance):
    devices = range(lax.axis_size(axis))
    route = [(i - distance, i) for i in devices if i - distance in devices]
    return lax.ppermute(block, axis, route)


def from_partner(value, axis, stride):
    mask = 2**stride
    pairs = [(source, source ^ mask) for source in range(lax.axis_size(axis))]
    return lax.ppermute(value, axis, pairs)


def pick_blocks(source, block_index):
    return lax.dynamic_slice_in_dim(source, block_index[0] * BLK, BLK, 0)


def _nt(a, b):
    return lax.dot_general(a, b, (((1,), (1,)), ((), ())), preferred_element_type=jnp.float32)


def _nn(a, b):
    return lax.dot_general(a, b, (((1,), (0,)), ((), ())), preferred_element_type=jnp.float32)


def attend_kernel(level_count, meta, q_ref, ok_ref, ov_ref, pk_ref, pv_ref, *rest):
    far_refs = rest[: 2 * level_count]
    out_ref, bias_ref = rest[-2:]
    rows = q_ref.shape[0]
    head_dim = HDIM
    panel_len = rows // BLK
    scale = head_dim ** (-0.5) * LOG2E

    @pl.when(pl.program_id(0) == 0)
    def _():
        row = lax.broadcasted_iota(jnp.int32, (rows, rows), 0)
        col = lax.broadcasted_iota(jnp.int32, (rows, rows), 1)
        q_blk = row // BLK
        k_blk = col // BLK
        width = jnp.zeros((rows, rows), jnp.int32)
        for r in range(panel_len):
            width = jnp.where(q_blk == r, meta[r], width)
        first_block = meta[panel_len]
        own_off = q_blk - k_blk
        own_vis = (own_off >= 0) & (own_off < width) & ((own_off > 0) | (col <= row))
        prev_off = q_blk + panel_len - k_blk
        prev_vis = (prev_off < width) & (first_block + q_blk - prev_off >= 0)
        bias_ref[:, :rows] = jnp.where(prev_vis, 0.0, -jnp.inf)
        bias_ref[:, rows:] = jnp.where(own_vis, 0.0, -jnp.inf)

    for sub in range(q_ref.shape[1] // head_dim):
        cols = slice(sub * head_dim, (sub + 1) * head_dim)
        q = q_ref[:, cols]
        s_prev = _nt(q, pk_ref[:, cols]) * scale + bias_ref[:, :rows]
        s_own = _nt(q, ok_ref[:, cols]) * scale + bias_ref[:, rows:]
        m_w = jnp.maximum(s_own.max(-1, keepdims=True), s_prev.max(-1, keepdims=True))
        e_own = jnp.exp2(s_own - m_w)
        e_prev = jnp.exp2(s_prev - m_w)
        l_w = e_own.sum(-1, keepdims=True) + e_prev.sum(-1, keepdims=True)
        o_w = _nn(e_own.astype(jnp.bfloat16), ov_ref[:, cols]) + _nn(e_prev.astype(jnp.bfloat16), pv_ref[:, cols])

        maxes, totals, sums = [m_w], [l_w], [o_w]
        for b in range(level_count):
            s = _nt(q, far_refs[2 * b][:, cols]) * scale
            m = s.max(-1, keepdims=True)
            e = jnp.exp2(s - m)
            maxes.append(m)
            totals.append(e.sum(-1, keepdims=True))
            sums.append(_nn(e.astype(jnp.bfloat16), far_refs[2 * b + 1][:, cols]))

        top = maxes[0]
        for m in maxes[1:]:
            top = jnp.maximum(top, m)
        total = jnp.zeros_like(l_w)
        output = jnp.zeros_like(o_w)
        for m, l, o in zip(maxes, totals, sums):
            factor = jnp.exp2(m - top)
            total = total + l * factor
            output = output + o * factor
        out_ref[:, cols] = (output / total).astype(out_ref.dtype)


def attend(meta, queries, own_k, own_v, prev_k, prev_v, far, first_head, prior=None):
    rows, features = queries.shape
    head_dim = features // HEADS
    block = head_dim * HEADS_PER_STEP
    heads = prev_k.shape[1] // block
    first_head = first_head // HEADS_PER_STEP
    level_count = len(far)
    far_rows = far[0].shape[0] // 2
    whole = pl.BlockSpec((rows, block), lambda h, meta: (0, h + first_head))
    part = pl.BlockSpec((rows, block), lambda h, meta: (0, h))
    far_specs = []
    for arrived in far:
        shift = first_head if arrived.shape[1] == features else 0
        far_specs.append(pl.BlockSpec((far_rows, block), lambda h, meta, shift=shift: (0, h + shift)))
        far_specs.append(pl.BlockSpec((far_rows, block), lambda h, meta, shift=shift: (1, h + shift)))
    far_args = []
    for arrived in far:
        far_args += [arrived, arrived]
    keys = 2 * rows + level_count * far_rows
    args = [meta, queries, own_k, own_v, prev_k, prev_v, *far_args]
    in_specs = [whole] * 3 + [part] * 2 + far_specs
    aliases = {}
    if prior is not None:
        aliases = {len(args): 0}
        args.append(prior)
        in_specs.append(pl.BlockSpec(memory_space=pl.ANY))
    return pl.pallas_call(
        functools.partial(attend_kernel, level_count),
        out_shape=jax.ShapeDtypeStruct((rows, features), queries.dtype),
        grid_spec=pltpu.PrefetchScalarGridSpec(
            num_scalar_prefetch=1,
            grid=(heads,),
            in_specs=in_specs,
            out_specs=whole,
            scratch_shapes=[pltpu.VMEM((rows, 2 * rows), jnp.float32)],
        ),
        input_output_aliases=aliases,
        compiler_params=pltpu.CompilerParams(dimension_semantics=("arbitrary",)),
        cost_estimate=pl.CostEstimate(
            flops=4 * rows * keys * head_dim * HEADS_PER_STEP * heads,
            transcendentals=rows * keys * heads * HEADS_PER_STEP,
            bytes_accessed=2 * head_dim * HEADS_PER_STEP * heads * (6 * rows + 2 * level_count * far_rows),
        ),
    )(*args)


def on_device(queries, key_rows, value_rows, widths, columns):
    token_count, features = queries.shape
    panel_len = token_count // BLK
    device = lax.axis_index("outer")
    level_count = lax.axis_size("outer").bit_length() - 1
    meta = jnp.concatenate([widths, (device * panel_len)[None]]).astype(jnp.int32)
    wanted = [columns[jnp.bitwise_xor(device, 1 << b), b] - device * panel_len for b in range(level_count)]
    width = features // CHUNKS
    context = None
    for c in range(CHUNKS):
        cols = slice(c * width, (c + 1) * width)
        prev_keys, prev_values = passed_along((key_rows[:, cols], value_rows[:, cols]), "outer", 1)
        far = [] if c == 0 else [level0]
        for level_bit in range(level_count):
            if level_bit == 0 and c > 0:
                continue
            cols_b = slice(0, features) if level_bit == 0 else cols
            outgoing = jnp.concatenate(
                [pick_blocks(key_rows, wanted[level_bit])[:, cols_b], pick_blocks(value_rows, wanted[level_bit])[:, cols_b]],
                axis=0,
            )
            far.append(from_partner(outgoing, "outer", level_bit))
            if level_bit == 0:
                level0 = far[0]
        context = attend(
            meta, queries, key_rows, value_rows, prev_keys, prev_values, far, c * (HEADS // CHUNKS), context
        )
    return context


def solution(mesh):
    placed = (
        P(("groups", "outer"), None),
        P(("groups", "outer"), None),
        P(("groups", "outer"), None),
        P(("groups", "outer")),
        P("groups", None, None),
    )
    return jax.shard_map(
        on_device,
        mesh=mesh,
        in_specs=placed,
        out_specs=P(("groups", "outer"), None),
        check_vma=False,
    )
```

```python
import functools

import jax
import jax.numpy as jnp
from jax import lax
from jax.experimental import pallas as pl
from jax.experimental.pallas import tpu as pltpu
from jax.sharding import PartitionSpec as P

HEADS = 16
BLK = 128
WIN = 4
HDIM = 128
LOG2E = 1.4426950408889634
HEADS_PER_STEP = 4
CHUNKS = 2


def passed_along(block, axis, distance):
    devices = range(lax.axis_size(axis))
    route = [(i - distance, i) for i in devices if i - distance in devices]
    return lax.ppermute(block, axis, route)


def from_partner(value, axis, stride):
    mask = 2**stride
    pairs = [(source, source ^ mask) for source in range(lax.axis_size(axis))]
    return lax.ppermute(value, axis, pairs)


def pick_blocks(source, block_index):
    return lax.dynamic_slice_in_dim(source, block_index[0] * BLK, BLK, 0)


def _nt(a, b):
    return lax.dot_general(a, b, (((1,), (1,)), ((), ())), preferred_element_type=jnp.float32)


def _nn(a, b):
    return lax.dot_general(a, b, (((1,), (0,)), ((), ())), preferred_element_type=jnp.float32)


def attend_kernel(level_count, meta, q_ref, ok_ref, ov_ref, pk_ref, pv_ref, *rest):
    far_refs = rest[: 2 * level_count]
    out_ref, bias_ref = rest[-2:]
    rows = q_ref.shape[0]
    head_dim = HDIM
    panel_len = rows // BLK
    scale = head_dim ** (-0.5) * LOG2E

    @pl.when(pl.program_id(0) == 0)
    def _():
        row = lax.broadcasted_iota(jnp.int32, (rows, rows), 0)
        col = lax.broadcasted_iota(jnp.int32, (rows, rows), 1)
        q_blk = row // BLK
        k_blk = col // BLK
        width = jnp.zeros((rows, rows), jnp.int32)
        for r in range(panel_len):
            width = jnp.where(q_blk == r, meta[r], width)
        first_block = meta[panel_len]
        own_off = q_blk - k_blk
        own_vis = (own_off >= 0) & (own_off < width) & ((own_off > 0) | (col <= row))
        prev_off = q_blk + panel_len - k_blk
        prev_vis = (prev_off < width) & (first_block + q_blk - prev_off >= 0)
        bias_ref[:, :rows] = jnp.where(prev_vis, 0.0, -jnp.inf)
        bias_ref[:, rows:] = jnp.where(own_vis, 0.0, -jnp.inf)

    for sub in range(q_ref.shape[1] // head_dim):
        cols = slice(sub * head_dim, (sub + 1) * head_dim)
        q = q_ref[:, cols]
        s_prev = _nt(q, pk_ref[:, cols]) * scale + bias_ref[:, :rows]
        s_own = _nt(q, ok_ref[:, cols]) * scale + bias_ref[:, rows:]
        m_w = jnp.maximum(s_own.max(-1, keepdims=True), s_prev.max(-1, keepdims=True))
        e_own = jnp.exp2(s_own - m_w)
        e_prev = jnp.exp2(s_prev - m_w)
        l_w = e_own.sum(-1, keepdims=True) + e_prev.sum(-1, keepdims=True)
        o_w = _nn(e_own.astype(jnp.bfloat16), ov_ref[:, cols]) + _nn(e_prev.astype(jnp.bfloat16), pv_ref[:, cols])

        maxes, totals, sums = [m_w], [l_w], [o_w]
        for b in range(level_count):
            s = _nt(q, far_refs[2 * b][:, cols]) * scale
            m = s.max(-1, keepdims=True)
            e = jnp.exp2(s - m)
            maxes.append(m)
            totals.append(e.sum(-1, keepdims=True))
            sums.append(_nn(e.astype(jnp.bfloat16), far_refs[2 * b + 1][:, cols]))

        top = maxes[0]
        for m in maxes[1:]:
            top = jnp.maximum(top, m)
        total = jnp.zeros_like(l_w)
        output = jnp.zeros_like(o_w)
        for m, l, o in zip(maxes, totals, sums):
            factor = jnp.exp2(m - top)
            total = total + l * factor
            output = output + o * factor
        out_ref[:, cols] = (output / total).astype(out_ref.dtype)


def attend(meta, queries, own_k, own_v, prev_k, prev_v, far, first_head, prior=None):
    rows, features = queries.shape
    head_dim = features // HEADS
    block = head_dim * HEADS_PER_STEP
    heads = prev_k.shape[1] // block
    first_head = first_head // HEADS_PER_STEP
    level_count = len(far)
    far_rows = far[0].shape[0] // 2
    whole = pl.BlockSpec((rows, block), lambda h, meta: (0, h + first_head))
    part = pl.BlockSpec((rows, block), lambda h, meta: (0, h))
    far_specs = []
    for _ in range(level_count):
        far_specs.append(pl.BlockSpec((far_rows, block), lambda h, meta: (0, h)))
        far_specs.append(pl.BlockSpec((far_rows, block), lambda h, meta: (1, h)))
    far_args = []
    for arrived in far:
        far_args += [arrived, arrived]
    keys = 2 * rows + level_count * far_rows
    args = [meta, queries, own_k, own_v, prev_k, prev_v, *far_args]
    in_specs = [whole] * 3 + [part] * 2 + far_specs
    aliases = {}
    if prior is not None:
        aliases = {len(args): 0}
        args.append(prior)
        in_specs.append(pl.BlockSpec(memory_space=pl.ANY))
    return pl.pallas_call(
        functools.partial(attend_kernel, level_count),
        out_shape=jax.ShapeDtypeStruct((rows, features), queries.dtype),
        grid_spec=pltpu.PrefetchScalarGridSpec(
            num_scalar_prefetch=1,
            grid=(heads,),
            in_specs=in_specs,
            out_specs=whole,
            scratch_shapes=[pltpu.VMEM((rows, 2 * rows), jnp.float32)],
        ),
        input_output_aliases=aliases,
        compiler_params=pltpu.CompilerParams(dimension_semantics=("arbitrary",)),
        cost_estimate=pl.CostEstimate(
            flops=4 * rows * keys * head_dim * HEADS_PER_STEP * heads,
            transcendentals=rows * keys * heads * HEADS_PER_STEP,
            bytes_accessed=2 * head_dim * HEADS_PER_STEP * heads * (6 * rows + 2 * level_count * far_rows),
        ),
    )(*args)


def on_device(queries, key_rows, value_rows, widths, columns):
    token_count, features = queries.shape
    panel_len = token_count // BLK
    device = lax.axis_index("outer")
    level_count = lax.axis_size("outer").bit_length() - 1
    meta = jnp.concatenate([widths, (device * panel_len)[None]]).astype(jnp.int32)
    wanted = [columns[jnp.bitwise_xor(device, 1 << b), b] - device * panel_len for b in range(level_count)]
    width = features // CHUNKS
    context = None
    held = ()
    for c in range(CHUNKS):
        cols = slice(c * width, (c + 1) * width)
        rim_keys, rim_values, *_ = lax.optimization_barrier((key_rows, value_rows, *held))
        prev_keys, prev_values = passed_along((rim_keys[:, cols], rim_values[:, cols]), "outer", 1)
        far = []
        for level_bit in range(level_count):
            outgoing = jnp.concatenate(
                [pick_blocks(key_rows, wanted[level_bit])[:, cols], pick_blocks(value_rows, wanted[level_bit])[:, cols]],
                axis=0,
            )
            far.append(from_partner(outgoing, "outer", level_bit))
        context = attend(
            meta, queries, key_rows, value_rows, prev_keys, prev_values, far, c * (HEADS // CHUNKS), context
        )
        held = (far[-1],)
    return context


def solution(mesh):
    placed = (
        P(("groups", "outer"), None),
        P(("groups", "outer"), None),
        P(("groups", "outer"), None),
        P(("groups", "outer")),
        P("groups", None, None),
    )
    return jax.shard_map(
        on_device,
        mesh=mesh,
        in_specs=placed,
        out_specs=P(("groups", "outer"), None),
        check_vma=False,
    )
```

```python
import functools

import jax
import jax.numpy as jnp
from jax import lax
from jax.experimental import pallas as pl
from jax.experimental.pallas import tpu as pltpu
from jax.sharding import PartitionSpec as P

HEADS = 16
BLK = 128
WIN = 4
HDIM = 128
LOG2E = 1.4426950408889634
HEADS_PER_STEP = 8
CHUNKS = 2


def passed_along(block, axis, distance):
    devices = range(lax.axis_size(axis))
    route = [(i - distance, i) for i in devices if i - distance in devices]
    return lax.ppermute(block, axis, route)


def from_partner(value, axis, stride):
    mask = 2**stride
    pairs = [(source, source ^ mask) for source in range(lax.axis_size(axis))]
    return lax.ppermute(value, axis, pairs)


def pick_blocks(source, block_index):
    return lax.dynamic_slice_in_dim(source, block_index[0] * BLK, BLK, 0)


def _nt(a, b):
    return lax.dot_general(a, b, (((1,), (1,)), ((), ())), preferred_element_type=jnp.float32)


def _nn(a, b):
    return lax.dot_general(a, b, (((1,), (0,)), ((), ())), preferred_element_type=jnp.float32)


def attend_kernel(level_count, meta, q_ref, ok_ref, ov_ref, pk_ref, pv_ref, *rest):
    far_refs = rest[: 2 * level_count]
    out_ref, bias_ref = rest[-2:]
    rows = q_ref.shape[0]
    head_dim = HDIM
    panel_len = rows // BLK
    scale = head_dim ** (-0.5) * LOG2E

    @pl.when(pl.program_id(0) == 0)
    def _():
        row = lax.broadcasted_iota(jnp.int32, (rows, rows), 0)
        col = lax.broadcasted_iota(jnp.int32, (rows, rows), 1)
        q_blk = row // BLK
        k_blk = col // BLK
        width = jnp.zeros((rows, rows), jnp.int32)
        for r in range(panel_len):
            width = jnp.where(q_blk == r, meta[r], width)
        first_block = meta[panel_len]
        own_off = q_blk - k_blk
        own_vis = (own_off >= 0) & (own_off < width) & ((own_off > 0) | (col <= row))
        prev_off = q_blk + panel_len - k_blk
        prev_vis = (prev_off < width) & (first_block + q_blk - prev_off >= 0)
        bias_ref[:, :rows] = jnp.where(prev_vis, 0.0, -jnp.inf)
        bias_ref[:, rows:] = jnp.where(own_vis, 0.0, -jnp.inf)

    for sub in range(q_ref.shape[1] // head_dim):
        cols = slice(sub * head_dim, (sub + 1) * head_dim)
        q = q_ref[:, cols]
        s_prev = _nt(q, pk_ref[:, cols]) * scale + bias_ref[:, :rows]
        s_own = _nt(q, ok_ref[:, cols]) * scale + bias_ref[:, rows:]
        m_w = jnp.maximum(s_own.max(-1, keepdims=True), s_prev.max(-1, keepdims=True))
        e_own = jnp.exp2(s_own - m_w)
        e_prev = jnp.exp2(s_prev - m_w)
        l_w = e_own.sum(-1, keepdims=True) + e_prev.sum(-1, keepdims=True)
        o_w = _nn(e_own.astype(jnp.bfloat16), ov_ref[:, cols]) + _nn(e_prev.astype(jnp.bfloat16), pv_ref[:, cols])

        maxes, totals, sums = [m_w], [l_w], [o_w]
        for b in range(level_count):
            s = _nt(q, far_refs[2 * b][:, cols]) * scale
            m = s.max(-1, keepdims=True)
            e = jnp.exp2(s - m)
            maxes.append(m)
            totals.append(e.sum(-1, keepdims=True))
            sums.append(_nn(e.astype(jnp.bfloat16), far_refs[2 * b + 1][:, cols]))

        top = maxes[0]
        for m in maxes[1:]:
            top = jnp.maximum(top, m)
        total = jnp.zeros_like(l_w)
        output = jnp.zeros_like(o_w)
        for m, l, o in zip(maxes, totals, sums):
            factor = jnp.exp2(m - top)
            total = total + l * factor
            output = output + o * factor
        out_ref[:, cols] = (output / total).astype(out_ref.dtype)


def attend(meta, queries, own_k, own_v, prev_k, prev_v, far, first_head, prior=None):
    rows, features = queries.shape
    head_dim = features // HEADS
    block = head_dim * HEADS_PER_STEP
    heads = prev_k.shape[1] // block
    first_head = first_head // HEADS_PER_STEP
    level_count = len(far)
    far_rows = far[0].shape[0] // 2
    whole = pl.BlockSpec((rows, block), lambda h, meta: (0, h + first_head))
    part = pl.BlockSpec((rows, block), lambda h, meta: (0, h))
    far_specs = []
    for _ in range(level_count):
        far_specs.append(pl.BlockSpec((far_rows, block), lambda h, meta: (0, h)))
        far_specs.append(pl.BlockSpec((far_rows, block), lambda h, meta: (1, h)))
    far_args = []
    for arrived in far:
        far_args += [arrived, arrived]
    keys = 2 * rows + level_count * far_rows
    args = [meta, queries, own_k, own_v, prev_k, prev_v, *far_args]
    in_specs = [whole] * 3 + [part] * 2 + far_specs
    aliases = {}
    if prior is not None:
        aliases = {len(args): 0}
        args.append(prior)
        in_specs.append(pl.BlockSpec(memory_space=pl.ANY))
    return pl.pallas_call(
        functools.partial(attend_kernel, level_count),
        out_shape=jax.ShapeDtypeStruct((rows, features), queries.dtype),
        grid_spec=pltpu.PrefetchScalarGridSpec(
            num_scalar_prefetch=1,
            grid=(heads,),
            in_specs=in_specs,
            out_specs=whole,
            scratch_shapes=[pltpu.VMEM((rows, 2 * rows), jnp.float32)],
        ),
        input_output_aliases=aliases,
        compiler_params=pltpu.CompilerParams(dimension_semantics=("arbitrary",)),
        cost_estimate=pl.CostEstimate(
            flops=4 * rows * keys * head_dim * HEADS_PER_STEP * heads,
            transcendentals=rows * keys * heads * HEADS_PER_STEP,
            bytes_accessed=2 * head_dim * HEADS_PER_STEP * heads * (6 * rows + 2 * level_count * far_rows),
        ),
    )(*args)


def on_device(queries, key_rows, value_rows, widths, columns):
    token_count, features = queries.shape
    panel_len = token_count // BLK
    device = lax.axis_index("outer")
    level_count = lax.axis_size("outer").bit_length() - 1
    meta = jnp.concatenate([widths, (device * panel_len)[None]]).astype(jnp.int32)
    wanted = [columns[jnp.bitwise_xor(device, 1 << b), b] - device * panel_len for b in range(level_count)]
    width = features // CHUNKS
    context = None
    for c in range(CHUNKS):
        cols = slice(c * width, (c + 1) * width)
        prev_keys, prev_values = passed_along((key_rows[:, cols], value_rows[:, cols]), "outer", 1)
        far = []
        for level_bit in range(level_count):
            outgoing = jnp.concatenate(
                [pick_blocks(key_rows, wanted[level_bit])[:, cols], pick_blocks(value_rows, wanted[level_bit])[:, cols]],
                axis=0,
            )
            far.append(from_partner(outgoing, "outer", level_bit))
        context = attend(
            meta, queries, key_rows, value_rows, prev_keys, prev_values, far, c * (HEADS // CHUNKS), context
        )
    return context


def solution(mesh):
    placed = (
        P(("groups", "outer"), None),
        P(("groups", "outer"), None),
        P(("groups", "outer"), None),
        P(("groups", "outer")),
        P("groups", None, None),
    )
    return jax.shard_map(
        on_device,
        mesh=mesh,
        in_specs=placed,
        out_specs=P(("groups", "outer"), None),
        check_vma=False,
    )
```
